32 devices in a mesh: groups: 2 (over y), clus: 4 (over z), pair: 2 (over x), rhs: 2 (over core).
Axes of the slice: x: 2, y: 2, z: 4, core: 2. Of those that a mesh axis runs over, the one named last changes fastest.
Arguments:
- rhs_field: float32 [16, 16384], P('rhs', ('groups', 'clus')), parts along dimension 1, may hold values from -6 to 6
- coefficients: float32 [4], replicated, may hold values from -1 to 1
- near_blocks: bfloat16 [256, 256, 256], P(('groups', 'clus', 'pair')), parts along dimension 0, may hold values from -0.125 to 0.125
- near_tgt: int32 [256], P(('groups', 'clus', 'pair')), parts along dimension 0, may hold values from 0 to 31, as said below
- near_src: int32 [256], P(('groups', 'clus', 'pair')), parts along dimension 0, may hold values from 0 to 31, as said below
- row_basis: bfloat16 [64, 16, 256], P(('groups', 'clus')), parts along dimension 0, may hold values from -0.25 to 0.25
- col_basis: bfloat16 [1024, 16, 256], P(('groups', 'clus', 'pair')), parts along dimension 0, may hold values from -0.375 to 0.375
- far_src: int32 [1024], P(('groups', 'clus', 'pair')), parts along dimension 0, may hold values from 0 to 31, as said below
- far_tgt: int32 [1024], P(('groups', 'clus', 'pair')), parts along dimension 0, may hold values from 0 to 31, as said below
Outputs:
- preconditioned: float32 [16, 16384], P('rhs', ('groups', 'clus')), parts along dimension 1
The draws below stay inside these ranges and needn't reach their ends.
There are 2 independent parts, one for each index of `groups`. The reference program is written for one: setup_inputs(seed, part) draws one part's arguments, and reference() takes and returns one part's arrays. A program takes and returns all parts, laid end to end along the dimension named above; an argument that names none is the same for every part. Nothing has to cross between parts.
Inputs may be any that keep to these rules, and one draw needn't show every extreme that they name: `near_tgt`: the rows are in aligned blocks of 16, one a device in the order of clus then pair; the block of clus index c names clusters c * 8 to (c + 1) * 8 - 1. `near_src`: in each aligned block of 16 rows (one a device, clus then pair, clus index c), exactly 2 rows name clusters of clus index c - 1 and exactly 2 name clusters of clus index c + 1 (both taken modulo the number of clus indices; cluster // 8 is a cluster's clus index), and all others name clusters of clus index c. `far_src`: the rows are in aligned blocks of 64, one a device in the order of clus then pair; the block of clus index c names clusters c * 8 to (c + 1) * 8 - 1. `far_tgt`: never equal to far_src of the same row.
All inputs are finite; a program needn't handle non-finite values.
Results may differ from the reference program's by a relative error of at most 0.0047.
Values may be sent and summed in bfloat16 or wider, within the bound.
No kernel may reach another device: no remote copies, remote signals or barrier semaphores. Data moves between devices by JAX's collectives and lax.ppermute only.
A program may use at most 64 MiB of HBM per device.

```python
import jax
import jax.numpy as jnp
from jax import lax

LEAF = 256
R = 16
RHS = 16
DEG = 3
CL_DEV = 8
NB_DEV = 16
NF_DEV = 64
NCL = 32
PANELS = 8192
NNEAR = 128
NFAR = 512
CAP = 2
NEAR_PER = 4
FAR_PER = 16
N_CLUS = 4
N_PAIR = 2


def draw_near_tgt(key, part):
    owner_index = jnp.arange(NNEAR) // (NB_DEV * N_PAIR)
    chosen = jax.random.randint(jax.random.fold_in(key, 11), (NNEAR,), 0, CL_DEV)
    return (owner_index * CL_DEV + chosen).astype(jnp.int32)


def draw_near_src(key, part):
    device_total = N_CLUS * N_PAIR
    own_index = jnp.arange(device_total) // N_PAIR
    local_count = NB_DEV - 2 * CAP
    own_ids = jnp.broadcast_to(own_index[:, None], (device_total, local_count))
    down_ids = jnp.broadcast_to(((own_index + N_CLUS - 1) % N_CLUS)[:, None], (device_total, CAP))
    up_ids = jnp.broadcast_to(((own_index + 1) % N_CLUS)[:, None], (device_total, CAP))
    device_ids = jnp.concatenate([own_ids, down_ids, up_ids], axis=1)
    second_keys = jax.random.split(jax.random.fold_in(key, 29), device_total)
    arrange = jax.vmap(lambda sub_key: jax.random.permutation(sub_key, NB_DEV))(second_keys)
    device_ids = jnp.take_along_axis(device_ids, arrange, axis=1)
    chosen = jax.random.randint(jax.random.fold_in(key, 31), (device_total, NB_DEV), 0, CL_DEV)
    return (device_ids * CL_DEV + chosen).reshape(NNEAR).astype(jnp.int32)


def far_pairs(key):
    owner_index = jnp.arange(NFAR) // (NF_DEV * N_PAIR)
    chosen = jax.random.randint(jax.random.fold_in(key, 41), (NFAR,), 0, CL_DEV)
    anchor = owner_index * CL_DEV + chosen
    offset = jax.random.randint(jax.random.fold_in(key, 43), (NFAR,), 1, NCL)
    target = (anchor + offset) % NCL
    return (anchor.astype(jnp.int32), target.astype(jnp.int32))


def draw_far_src(key, part):
    return far_pairs(key)[0]


def draw_far_tgt(key, part):
    return far_pairs(key)[1]


def levels(rng, shape, pieces, low, high):
    def one(dim, parts):
        heights = jax.random.uniform(jax.random.fold_in(jax.random.fold_in(rng, 6), dim), (parts,), jnp.float32, low / len(pieces), high / len(pieces))
        return jnp.repeat(jnp.exp(heights), shape[dim] // parts).reshape((-1,) + (1,) * (len(shape) - dim - 1))

    loudness = one(*pieces[0])
    for cut in pieces[1:]:
        loudness = loudness * one(*cut)
    return loudness


def bell_draw(stream_key, extent, deviation, most, pieces=(), dtype=jnp.bfloat16):
    loudness = levels(stream_key, extent, pieces, -0.22, 0.18) if pieces else 1.0
    values = jax.random.normal(stream_key, extent, jnp.float32) * deviation * loudness
    return jnp.minimum(jnp.maximum(values, -most), most).astype(dtype)


def setup_inputs(seed: int = 0, part: int = 0) -> dict:
    streams_of = jax.random.split(jax.random.key(seed), 10)
    own_keys = jax.random.split(jax.random.fold_in(streams_of[9], part), 10)
    rhs_field = bell_draw(own_keys[0], (RHS, PANELS), 1.0, 6.0, ((0, 2), (1, 4)), jnp.float32)
    coefficients = jnp.clip(jax.random.uniform(streams_of[1], (DEG + 1,), jnp.float32, -1.0, 1.0), -1.0, 1.0)
    near_blocks = bell_draw(own_keys[2], (NNEAR, LEAF, LEAF), (2 * LEAF * NEAR_PER) ** -0.5, 0.125, ((0, 8),))
    near_tgt = draw_near_tgt(jax.random.fold_in(jax.random.fold_in(streams_of[9], part), 71), part)
    near_src = draw_near_src(jax.random.fold_in(jax.random.fold_in(streams_of[9], part), 71), part)
    row_basis = bell_draw(own_keys[5], (NCL, R, LEAF), (2 * R * FAR_PER) ** -0.5, 0.25, ((0, 4),))
    col_basis = bell_draw(own_keys[6], (NFAR, R, LEAF), LEAF ** -0.5, 0.375, ((0, 8),))
    far_src = draw_far_src(jax.random.fold_in(jax.random.fold_in(streams_of[9], part), 71), part)
    far_tgt = draw_far_tgt(jax.random.fold_in(jax.random.fold_in(streams_of[9], part), 71), part)
    return dict(rhs_field=rhs_field, coefficients=coefficients, near_blocks=near_blocks, near_tgt=near_tgt, near_src=near_src, row_basis=row_basis, col_basis=col_basis, far_src=far_src, far_tgt=far_tgt)


def reference(rhs_field, coefficients, near_blocks, near_tgt, near_src, row_basis, col_basis, far_src, far_tgt):
    source = rhs_field.reshape(RHS, NCL, LEAF)
    iterate = (coefficients[DEG] * source).astype(jnp.bfloat16)
    groups_count = NNEAR // NB_DEV
    blocks = near_blocks.reshape(groups_count, NB_DEV, LEAF, LEAF)
    targets = near_tgt.reshape(groups_count, NB_DEV).astype(jnp.int32)
    anchors = near_src.reshape(groups_count, NB_DEV).astype(jnp.int32)
    result = source
    for step in range(DEG):
        degree = DEG - 1 - step
        current = iterate

        def near_step(total, item):
            block_set, target_set, anchor_set = item
            gathered = current[:, anchor_set, :].astype(jnp.float32)
            partial_value = jnp.einsum("rjs,jts->rjt", gathered, block_set.astype(jnp.float32), precision=lax.Precision.HIGHEST)
            return total.at[:, target_set, :].add(partial_value), None

        near, unused = lax.scan(near_step, jnp.zeros((RHS, NCL, LEAF), jnp.float32), (blocks, targets, anchors))
        far_input = current[:, far_src, :].astype(jnp.float32)
        coef = jnp.einsum("rjl,jkl->rjk", far_input, col_basis.astype(jnp.float32), precision=lax.Precision.HIGHEST)
        sums = jnp.zeros((RHS, NCL, R), jnp.float32).at[:, far_tgt, :].add(coef)
        far = jnp.einsum("rck,ckl->rcl", sums, row_basis.astype(jnp.float32), precision=lax.Precision.HIGHEST)
        result = near + far + coefficients[degree] * source
        iterate = result.astype(jnp.bfloat16)
    return result.reshape(RHS, PANELS)
```

```python
import jax
import jax.numpy as jnp
from jax import lax
from jax.sharding import PartitionSpec as P


def shift(value, axis, count, step):
    return lax.ppermute(value, axis, [(i, (i + step) % count) for i in range(count)])


def pair_total(value, pair_count, pair_index):
    if pair_count == 1:
        return value
    if pair_count == 2:
        return value + shift(value, "pair", 2, 1)
    received = [value] + [shift(value, "pair", pair_count, s) for s in range(1, pair_count)]
    stacked = jnp.stack(received)
    order = (pair_index - jnp.arange(pair_count)) % pair_count
    canonical = stacked[order]
    total = canonical[0]
    for q in range(1, pair_count):
        total = total + canonical[q]
    return total


def shards(
    rhs_field, coefficients, near_blocks, near_tgt, near_src, row_basis, col_basis, far_src, far_tgt
):
    rhs_here = rhs_field.shape[0]
    clusters_here = row_basis.shape[0]
    rank_size = row_basis.shape[1]
    leaf_size = row_basis.shape[2]
    peer_count = lax.axis_size("clus")
    pair_count = lax.axis_size("pair")
    cluster_count = clusters_here * peer_count
    degree_top = coefficients.shape[0] - 1
    my_index = lax.axis_index("clus")
    pair_index = lax.axis_index("pair")
    my_base = my_index * clusters_here
    source = rhs_field.reshape(rhs_here, clusters_here, leaf_size)

    target_local = near_tgt - my_base
    target_hot = (target_local[:, None] == jnp.arange(clusters_here)[None, :]).astype(jnp.float32)
    relative = (near_src // clusters_here - my_index) % peer_count
    slot = jnp.where(relative == 0, 0, jnp.where(relative == 1, 1, 2))
    near_index = slot * clusters_here + near_src % clusters_here

    far_local = far_src - my_base
    far_hot = (far_tgt[:, None] == jnp.arange(cluster_count)[None, :]).astype(jnp.float32)
    row_f32 = row_basis.astype(jnp.float32)

    iterate = (coefficients[degree_top] * source).astype(jnp.bfloat16)
    result = source
    for step in range(degree_top):
        degree = degree_top - 1 - step
        with jax.named_scope("neighbour_iterates"):
            if peer_count > 1:
                from_minus = shift(iterate, "clus", peer_count, 1)
                from_plus = shift(iterate, "clus", peer_count, peer_count - 1)
            else:
                from_minus = iterate
                from_plus = iterate
        with jax.named_scope("far_partial"):
            far_input = iterate[:, far_local, :]
            coef = jnp.einsum(
                "rjl,jkl->jrk", far_input, col_basis, preferred_element_type=jnp.float32
            )
            coef = coef.reshape(coef.shape[0], rhs_here * rank_size)
            partial_value = jnp.einsum("jc,jm->cm", far_hot, coef, precision=lax.Precision.HIGHEST)
            partial_value = partial_value.reshape(peer_count, clusters_here, rhs_here * rank_size)
        with jax.named_scope("far_slices"):
            far_mine = partial_value[my_index]
            for s in range(1, peer_count):
                outgoing = partial_value[(my_index + s) % peer_count]
                far_mine = far_mine + shift(outgoing, "clus", peer_count, s)
        with jax.named_scope("near_partial"):
            extended = jnp.concatenate([iterate, from_plus, from_minus], axis=1)
            gathered = extended[:, near_index, :]
            contrib = jnp.einsum(
                "rjs,jts->rjt", gathered, near_blocks, preferred_element_type=jnp.float32
            )
            near_part = jnp.einsum(
                "rjt,jc->rct", contrib, target_hot, precision=lax.Precision.HIGHEST
            )
        with jax.named_scope("pair_sums"):
            near_flat = near_part.reshape(rhs_here, clusters_here * leaf_size)
            far_flat = far_mine.reshape(clusters_here, rhs_here, rank_size)
            far_flat = far_flat.transpose(1, 0, 2).reshape(rhs_here, clusters_here * rank_size)
            packed = jnp.concatenate([near_flat, far_flat], axis=1)
            packed = pair_total(packed, pair_count, pair_index)
            near_sum = packed[:, : clusters_here * leaf_size].reshape(
                rhs_here, clusters_here, leaf_size
            )
            coef_sum = packed[:, clusters_here * leaf_size :].reshape(
                rhs_here, clusters_here, rank_size
            )
        with jax.named_scope("far_field"):
            far_field = jnp.einsum(
                "rck,ckl->rcl", coef_sum, row_f32, precision=lax.Precision.HIGHEST
            )
        result = near_sum + far_field + coefficients[degree] * source
        iterate = result.astype(jnp.bfloat16)
    return result.reshape(rhs_here, clusters_here * leaf_size)


def solution(mesh):
    return jax.shard_map(
        shards,
        mesh=mesh,
        in_specs=(
            P("rhs", ("groups", "clus")),
            P(),
            P(("groups", "clus", "pair"), None, None),
            P(("groups", "clus", "pair")),
            P(("groups", "clus", "pair")),
            P(("groups", "clus"), None, None),
            P(("groups", "clus", "pair"), None, None),
            P(("groups", "clus", "pair")),
            P(("groups", "clus", "pair")),
        ),
        out_specs=P("rhs", ("groups", "clus")),
        check_vma=False,
    )
```

```python
import jax
import jax.numpy as jnp
from jax import lax
from jax.sharding import PartitionSpec as P


def shift(value, axis, count, step):
    return lax.ppermute(value, axis, [(i, (i + step) % count) for i in range(count)])


def pair_total(value, pair_count, pair_index):
    if pair_count == 1:
        return value
    if pair_count == 2:
        return value + shift(value, "pair", 2, 1)
    received = [value] + [shift(value, "pair", pair_count, s) for s in range(1, pair_count)]
    stacked = jnp.stack(received)
    order = (pair_index - jnp.arange(pair_count)) % pair_count
    canonical = stacked[order]
    total = canonical[0]
    for q in range(1, pair_count):
        total = total + canonical[q]
    return total


def shards(
    rhs_field, coefficients, near_blocks, near_tgt, near_src, row_basis, col_basis, far_src, far_tgt
):
    rhs_here = rhs_field.shape[0]
    clusters_here = row_basis.shape[0]
    rank_size = row_basis.shape[1]
    leaf_size = row_basis.shape[2]
    peer_count = lax.axis_size("clus")
    pair_count = lax.axis_size("pair")
    cluster_count = clusters_here * peer_count
    degree_top = coefficients.shape[0] - 1
    my_index = lax.axis_index("clus")
    pair_index = lax.axis_index("pair")
    my_base = my_index * clusters_here
    source = rhs_field.reshape(rhs_here, clusters_here, leaf_size)

    target_local = near_tgt - my_base
    target_hot = (target_local[:, None] == jnp.arange(clusters_here)[None, :]).astype(jnp.float32)
    relative = (near_src // clusters_here - my_index) % peer_count
    slot = jnp.where(relative == 0, 0, jnp.where(relative == 1, 1, 2))
    near_index = slot * clusters_here + near_src % clusters_here

    far_local = far_src - my_base
    far_hot = (far_tgt[:, None] == jnp.arange(cluster_count)[None, :]).astype(jnp.float32)
    row_f32 = row_basis.astype(jnp.float32)

    iterate = (coefficients[degree_top] * source).astype(jnp.bfloat16)
    result = source
    for step in range(degree_top):
        degree = degree_top - 1 - step
        with jax.named_scope("far_partial"):
            far_input = iterate[:, far_local, :]
            coef = jnp.einsum(
                "rjl,jkl->jrk", far_input, col_basis, preferred_element_type=jnp.float32
            )
            coef = coef.reshape(coef.shape[0], rhs_here * rank_size)
            partial_value = jnp.einsum("jc,jm->cm", far_hot, coef, precision=lax.Precision.HIGHEST)
            partial_value = partial_value.reshape(peer_count, clusters_here, rhs_here, rank_size)
            partial_value = partial_value.transpose(0, 2, 1, 3).reshape(
                peer_count, rhs_here, clusters_here * rank_size
            )
        with jax.named_scope("clus_exchange"):
            far_mine = partial_value[my_index]
            iterate_wide = iterate.reshape(rhs_here, clusters_here * leaf_size).astype(jnp.float32)
            iterate_size = clusters_here * leaf_size
            from_minus = iterate
            from_plus = iterate
            for s in range(1, peer_count):
                outgoing = partial_value[(my_index + s) % peer_count]
                carries_iterate = s == 1 or s == peer_count - 1
                if carries_iterate:
                    outgoing = jnp.concatenate([iterate_wide, outgoing], axis=1)
                incoming = shift(outgoing, "clus", peer_count, s)
                if carries_iterate:
                    neighbour = incoming[:, :iterate_size].astype(jnp.bfloat16)
                    neighbour = neighbour.reshape(rhs_here, clusters_here, leaf_size)
                    if s == 1:
                        from_minus = neighbour
                    if s == peer_count - 1:
                        from_plus = neighbour
                    incoming = incoming[:, iterate_size:]
                far_mine = far_mine + incoming
        with jax.named_scope("near_partial"):
            extended = jnp.concatenate([iterate, from_plus, from_minus], axis=1)
            gathered = extended[:, near_index, :]
            contrib = jnp.einsum(
                "rjs,jts->rjt", gathered, near_blocks, preferred_element_type=jnp.float32
            )
            near_part = jnp.einsum(
                "rjt,jc->rct", contrib, target_hot, precision=lax.Precision.HIGHEST
            )
        with jax.named_scope("pair_sums"):
            near_flat = near_part.reshape(rhs_here, clusters_here * leaf_size)
            packed = jnp.concatenate([near_flat, far_mine], axis=1)
            packed = pair_total(packed, pair_count, pair_index)
            near_sum = packed[:, : clusters_here * leaf_size].reshape(
                rhs_here, clusters_here, leaf_size
            )
            coef_sum = packed[:, clusters_here * leaf_size :].reshape(
                rhs_here, clusters_here, rank_size
            )
        with jax.named_scope("far_field"):
            far_field = jnp.einsum(
                "rck,ckl->rcl", coef_sum, row_f32, precision=lax.Precision.HIGHEST
            )
        result = near_sum + far_field + coefficients[degree] * source
        iterate = result.astype(jnp.bfloat16)
    return result.reshape(rhs_here, clusters_here * leaf_size)


def solution(mesh):
    return jax.shard_map(
        shards,
        mesh=mesh,
        in_specs=(
            P("rhs", ("groups", "clus")),
            P(),
            P(("groups", "clus", "pair"), None, None),
            P(("groups", "clus", "pair")),
            P(("groups", "clus", "pair")),
            P(("groups", "clus"), None, None),
            P(("groups", "clus", "pair"), None, None),
            P(("groups", "clus", "pair")),
            P(("groups", "clus", "pair")),
        ),
        out_specs=P("rhs", ("groups", "clus")),
        check_vma=False,
    )
```

```python
import jax
import jax.numpy as jnp
from jax import lax
from jax.sharding import PartitionSpec as P


def shift(value, axis, count, step):
    return lax.ppermute(value, axis, [(i, (i + step) % count) for i in range(count)])


def pair_total(value, pair_count, pair_index):
    if pair_count == 1:
        return value
    if pair_count == 2:
        return value + shift(value, "pair", 2, 1)
    received = [value] + [shift(value, "pair", pair_count, s) for s in range(1, pair_count)]
    stacked = jnp.stack(received)
    order = (pair_index - jnp.arange(pair_count)) % pair_count
    canonical = stacked[order]
    total = canonical[0]
    for q in range(1, pair_count):
        total = total + canonical[q]
    return total


def shards(
    rhs_field, coefficients, near_blocks, near_tgt, near_src, row_basis, col_basis, far_src, far_tgt
):
    rhs_here = rhs_field.shape[0]
    clusters_here = row_basis.shape[0]
    rank_size = row_basis.shape[1]
    leaf_size = row_basis.shape[2]
    peer_count = lax.axis_size("clus")
    pair_count = lax.axis_size("pair")
    cluster_count = clusters_here * peer_count
    degree_top = coefficients.shape[0] - 1
    my_index = lax.axis_index("clus")
    pair_index = lax.axis_index("pair")
    my_base = my_index * clusters_here
    source = rhs_field.reshape(rhs_here, clusters_here, leaf_size)

    target_local = near_tgt - my_base
    target_hot = (target_local[:, None] == jnp.arange(clusters_here)[None, :]).astype(jnp.float32)
    relative = (near_src // clusters_here - my_index) % peer_count
    slot = jnp.where(relative == 0, 0, jnp.where(relative == 1, 1, 2))
    near_index = slot * clusters_here + near_src % clusters_here

    far_local = far_src - my_base
    far_hot = (far_tgt[:, None] == jnp.arange(cluster_count)[None, :]).astype(jnp.float32)
    row_f32 = row_basis.astype(jnp.float32)

    stream_count = 2 if rhs_here % 2 == 0 else 1
    rhs_stream = rhs_here // stream_count

    def product(iterate, source_part, degree):
        with jax.named_scope("far_partial"):
            far_input = iterate[:, far_local, :]
            coef = jnp.einsum(
                "rjl,jkl->jrk", far_input, col_basis, preferred_element_type=jnp.float32
            )
            coef = coef.reshape(coef.shape[0], rhs_stream * rank_size)
            partial_value = jnp.einsum("jc,jm->cm", far_hot, coef, precision=lax.Precision.HIGHEST)
            partial_value = partial_value.reshape(peer_count, clusters_here, rhs_stream, rank_size)
            partial_value = partial_value.transpose(0, 2, 1, 3).reshape(
                peer_count, rhs_stream, clusters_here * rank_size
            )
        with jax.named_scope("clus_exchange"):
            far_mine = partial_value[my_index]
            iterate_wide = iterate.reshape(rhs_stream, clusters_here * leaf_size).astype(jnp.float32)
            iterate_size = clusters_here * leaf_size
            from_minus = iterate
            from_plus = iterate
            for s in range(1, peer_count):
                outgoing = partial_value[(my_index + s) % peer_count]
                carries_iterate = s == 1 or s == peer_count - 1
                if carries_iterate:
                    outgoing = jnp.concatenate([iterate_wide, outgoing], axis=1)
                incoming = shift(outgoing, "clus", peer_count, s)
                if carries_iterate:
                    neighbour = incoming[:, :iterate_size].astype(jnp.bfloat16)
                    neighbour = neighbour.reshape(rhs_stream, clusters_here, leaf_size)
                    if s == 1:
                        from_minus = neighbour
                    if s == peer_count - 1:
                        from_plus = neighbour
                    incoming = incoming[:, iterate_size:]
                far_mine = far_mine + incoming
        with jax.named_scope("near_partial"):
            extended = jnp.concatenate([iterate, from_plus, from_minus], axis=1)
            gathered = extended[:, near_index, :]
            contrib = jnp.einsum(
                "rjs,jts->rjt", gathered, near_blocks, preferred_element_type=jnp.float32
            )
            near_part = jnp.einsum(
                "rjt,jc->rct", contrib, target_hot, precision=lax.Precision.HIGHEST
            )
        with jax.named_scope("pair_sums"):
            near_flat = near_part.reshape(rhs_stream, clusters_here * leaf_size)
            packed = jnp.concatenate([near_flat, far_mine], axis=1)
            packed = pair_total(packed, pair_count, pair_index)
            near_sum = packed[:, : clusters_here * leaf_size].reshape(
                rhs_stream, clusters_here, leaf_size
            )
            coef_sum = packed[:, clusters_here * leaf_size :].reshape(
                rhs_stream, clusters_here, rank_size
            )
        with jax.named_scope("far_field"):
            far_field = jnp.einsum(
                "rck,ckl->rcl", coef_sum, row_f32, precision=lax.Precision.HIGHEST
            )
        return near_sum + far_field + coefficients[degree] * source_part

    sources = [source[k * rhs_stream : (k + 1) * rhs_stream] for k in range(stream_count)]
    iterates = [(coefficients[degree_top] * part).astype(jnp.bfloat16) for part in sources]
    results = sources
    for step in range(degree_top):
        degree = degree_top - 1 - step
        results = [product(iterates[k], sources[k], degree) for k in range(stream_count)]
        iterates = [part.astype(jnp.bfloat16) for part in results]
    result = jnp.concatenate(results, axis=0)
    return result.reshape(rhs_here, clusters_here * leaf_size)


def solution(mesh):
    return jax.shard_map(
        shards,
        mesh=mesh,
        in_specs=(
            P("rhs", ("groups", "clus")),
            P(),
            P(("groups", "clus", "pair"), None, None),
            P(("groups", "clus", "pair")),
            P(("groups", "clus", "pair")),
            P(("groups", "clus"), None, None),
            P(("groups", "clus", "pair"), None, None),
            P(("groups", "clus", "pair")),
            P(("groups", "clus", "pair")),
        ),
        out_specs=P("rhs", ("groups", "clus")),
        check_vma=False,
    )
```

```python
import jax
import jax.numpy as jnp
from jax import lax
from jax.sharding import PartitionSpec as P


def shift(value, axis, count, step):
    return lax.ppermute(value, axis, [(i, (i + step) % count) for i in range(count)])


def pair_total(value, pair_count, pair_index):
    if pair_count == 1:
        return value
    if pair_count == 2:
        return value + shift(value, "pair", 2, 1)
    received = [value] + [shift(value, "pair", pair_count, s) for s in range(1, pair_count)]
    stacked = jnp.stack(received)
    order = (pair_index - jnp.arange(pair_count)) % pair_count
    canonical = stacked[order]
    total = canonical[0]
    for q in range(1, pair_count):
        total = total + canonical[q]
    return total


def shards(
    rhs_field, coefficients, near_blocks, near_tgt, near_src, row_basis, col_basis, far_src, far_tgt
):
    rhs_here = rhs_field.shape[0]
    clusters_here = row_basis.shape[0]
    rank_size = row_basis.shape[1]
    leaf_size = row_basis.shape[2]
    peer_count = lax.axis_size("clus")
    pair_count = lax.axis_size("pair")
    cluster_count = clusters_here * peer_count
    degree_top = coefficients.shape[0] - 1
    my_index = lax.axis_index("clus")
    pair_index = lax.axis_index("pair")
    my_base = my_index * clusters_here
    source = rhs_field.reshape(rhs_here, clusters_here, leaf_size)

    target_local = near_tgt - my_base
    target_hot = (target_local[:, None] == jnp.arange(clusters_here)[None, :]).astype(jnp.float32)
    relative = (near_src // clusters_here - my_index) % peer_count
    slot = jnp.where(relative == 0, 0, jnp.where(relative == 1, 1, 2))
    near_index = slot * clusters_here + near_src % clusters_here
    near_pick = (near_index[:, None] == jnp.arange(3 * clusters_here)[None, :]).astype(jnp.bfloat16)

    far_local = far_src - my_base
    far_hot = (far_tgt[:, None] == jnp.arange(cluster_count)[None, :]).astype(jnp.float32)
    far_pick = (far_local[:, None] == jnp.arange(clusters_here)[None, :]).astype(jnp.bfloat16)
    row_f32 = row_basis.astype(jnp.float32)

    iterate = (coefficients[degree_top] * source).astype(jnp.bfloat16)
    result = source
    for step in range(degree_top):
        degree = degree_top - 1 - step
        with jax.named_scope("far_partial"):
            far_input = jnp.einsum(
                "jc,rcl->rjl", far_pick, iterate, preferred_element_type=jnp.bfloat16
            )
            coef = jnp.einsum(
                "rjl,jkl->jrk", far_input, col_basis, preferred_element_type=jnp.float32
            )
            coef = coef.reshape(coef.shape[0], rhs_here * rank_size)
            partial_value = jnp.einsum("jc,jm->cm", far_hot, coef, precision=lax.Precision.HIGHEST)
            partial_value = partial_value.reshape(peer_count, clusters_here, rhs_here, rank_size)
            partial_value = partial_value.transpose(0, 2, 1, 3).reshape(
                peer_count, rhs_here, clusters_here * rank_size
            )
        with jax.named_scope("clus_exchange"):
            far_mine = partial_value[my_index]
            iterate_wide = iterate.reshape(rhs_here, clusters_here * leaf_size).astype(jnp.float32)
            iterate_size = clusters_here * leaf_size
            from_minus = iterate
            from_plus = iterate
            for s in range(1, peer_count):
                outgoing = partial_value[(my_index + s) % peer_count]
                carries_iterate = s == 1 or s == peer_count - 1
                if carries_iterate:
                    outgoing = jnp.concatenate([iterate_wide, outgoing], axis=1)
                incoming = shift(outgoing, "clus", peer_count, s)
                if carries_iterate:
                    neighbour = incoming[:, :iterate_size].astype(jnp.bfloat16)
                    neighbour = neighbour.reshape(rhs_here, clusters_here, leaf_size)
                    if s == 1:
                        from_minus = neighbour
                    if s == peer_count - 1:
                        from_plus = neighbour
                    incoming = incoming[:, iterate_size:]
                far_mine = far_mine + incoming
        with jax.named_scope("near_partial"):
            extended = jnp.concatenate([iterate, from_plus, from_minus], axis=1)
            gathered = jnp.einsum(
                "jc,rcs->rjs", near_pick, extended, preferred_element_type=jnp.bfloat16
            )
            contrib = jnp.einsum(
                "rjs,jts->rjt", gathered, near_blocks, preferred_element_type=jnp.float32
            )
            near_part = jnp.einsum(
                "rjt,jc->rct", contrib, target_hot, precision=lax.Precision.HIGHEST
            )
        with jax.named_scope("pair_sums"):
            near_flat = near_part.reshape(rhs_here, clusters_here * leaf_size)
            packed = jnp.concatenate([near_flat, far_mine], axis=1)
            packed = pair_total(packed, pair_count, pair_index)
            near_sum = packed[:, : clusters_here * leaf_size].reshape(
                rhs_here, clusters_here, leaf_size
            )
            coef_sum = packed[:, clusters_here * leaf_size :].reshape(
                rhs_here, clusters_here, rank_size
            )
        with jax.named_scope("far_field"):
            far_field = jnp.einsum(
                "rck,ckl->rcl", coef_sum, row_f32, precision=lax.Precision.HIGHEST
            )
        source_late, near_sum = lax.optimization_barrier((source, near_sum))
        result = near_sum + far_field + coefficients[degree] * source_late
        iterate = result.astype(jnp.bfloat16)
    return result.reshape(rhs_here, clusters_here * leaf_size)


def solution(mesh):
    return jax.shard_map(
        shards,
        mesh=mesh,
        in_specs=(
            P("rhs", ("groups", "clus")),
            P(),
            P(("groups", "clus", "pair"), None, None),
            P(("groups", "clus", "pair")),
            P(("groups", "clus", "pair")),
            P(("groups", "clus"), None, None),
            P(("groups", "clus", "pair"), None, None),
            P(("groups", "clus", "pair")),
            P(("groups", "clus", "pair")),
        ),
        out_specs=P("rhs", ("groups", "clus")),
        check_vma=False,
    )
```

```python
import jax
import jax.numpy as jnp
from jax import lax
from jax.sharding import PartitionSpec as P


def shift(value, axis, count, step):
    return lax.ppermute(value, axis, [(i, (i + step) % count) for i in range(count)])


def pair_total(value, pair_count, pair_index):
    if pair_count == 1:
        return value
    if pair_count == 2:
        return value + shift(value, "pair", 2, 1)
    received = [value] + [shift(value, "pair", pair_count, s) for s in range(1, pair_count)]
    stacked = jnp.stack(received)
    order = (pair_index - jnp.arange(pair_count)) % pair_count
    canonical = stacked[order]
    total = canonical[0]
    for q in range(1, pair_count):
        total = total + canonical[q]
    return total


def shards(
    rhs_field, coefficients, near_blocks, near_tgt, near_src, row_basis, col_basis, far_src, far_tgt
):
    rhs_here = rhs_field.shape[0]
    clusters_here = row_basis.shape[0]
    rank_size = row_basis.shape[1]
    leaf_size = row_basis.shape[2]
    peer_count = lax.axis_size("clus")
    pair_count = lax.axis_size("pair")
    cluster_count = clusters_here * peer_count
    degree_top = coefficients.shape[0] - 1
    my_index = lax.axis_index("clus")
    pair_index = lax.axis_index("pair")
    my_base = my_index * clusters_here
    source = rhs_field.reshape(rhs_here, clusters_here, leaf_size)

    target_local = near_tgt - my_base
    target_hot = (target_local[:, None] == jnp.arange(clusters_here)[None, :]).astype(jnp.float32)
    relative = (near_src // clusters_here - my_index) % peer_count
    slot = jnp.where(relative == 0, 0, jnp.where(relative == 1, 1, 2))
    near_index = slot * clusters_here + near_src % clusters_here
    near_pick = (near_index[:, None] == jnp.arange(3 * clusters_here)[None, :]).astype(jnp.bfloat16)

    far_local = far_src - my_base
    far_hot = (far_tgt[:, None] == jnp.arange(cluster_count)[None, :]).astype(jnp.float32)
    far_pick = (far_local[:, None] == jnp.arange(clusters_here)[None, :]).astype(jnp.bfloat16)
    row_f32 = row_basis.astype(jnp.float32)

    iterate = (coefficients[degree_top] * source).astype(jnp.bfloat16)
    result = source
    scaled = None
    for step in range(degree_top):
        degree = degree_top - 1 - step
        with jax.named_scope("far_partial"):
            far_input = jnp.einsum(
                "jc,rcl->rjl", far_pick, iterate, preferred_element_type=jnp.bfloat16
            )
            coef = jnp.einsum(
                "rjl,jkl->jrk", far_input, col_basis, preferred_element_type=jnp.float32
            )
            coef = coef.reshape(coef.shape[0], rhs_here * rank_size)
            partial_value = jnp.einsum("jc,jm->cm", far_hot, coef, precision=lax.Precision.HIGH)
            partial_value = partial_value.reshape(peer_count, clusters_here, rhs_here, rank_size)
            partial_value = partial_value.transpose(0, 2, 1, 3).reshape(
                peer_count, rhs_here, clusters_here * rank_size
            )
        with jax.named_scope("clus_exchange"):
            far_mine = partial_value[my_index]
            iterate_wide = iterate.reshape(rhs_here, clusters_here * leaf_size).astype(jnp.float32)
            iterate_size = clusters_here * leaf_size
            from_minus = iterate
            from_plus = iterate
            for s in range(1, peer_count):
                outgoing = partial_value[(my_index + s) % peer_count]
                carries_iterate = s == 1 or s == peer_count - 1
                if carries_iterate:
                    outgoing = jnp.concatenate([iterate_wide, outgoing], axis=1)
                if scaled is None:
                    source_late, outgoing = lax.optimization_barrier((source, outgoing))
                    scaled = [coefficients[d] * source_late for d in range(degree_top)]
                incoming = shift(outgoing, "clus", peer_count, s)
                if carries_iterate:
                    neighbour = incoming[:, :iterate_size].astype(jnp.bfloat16)
                    neighbour = neighbour.reshape(rhs_here, clusters_here, leaf_size)
                    if s == 1:
                        from_minus = neighbour
                    if s == peer_count - 1:
                        from_plus = neighbour
                    incoming = incoming[:, iterate_size:]
                far_mine = far_mine + incoming
        with jax.named_scope("near_partial"):
            extended = jnp.concatenate([iterate, from_plus, from_minus], axis=1)
            gathered = jnp.einsum(
                "jc,rcs->rjs", near_pick, extended, preferred_element_type=jnp.bfloat16
            )
            contrib = jnp.einsum(
                "rjs,jts->rjt", gathered, near_blocks, preferred_element_type=jnp.float32
            )
            near_part = jnp.einsum(
                "rjt,jc->rct", contrib, target_hot, precision=lax.Precision.HIGH
            )
        with jax.named_scope("pair_sums"):
            near_flat = near_part.reshape(rhs_here, clusters_here * leaf_size)
            packed = jnp.concatenate([near_flat, far_mine], axis=1)
            packed = pair_total(packed, pair_count, pair_index)
            near_sum = packed[:, : clusters_here * leaf_size].reshape(
                rhs_here, clusters_here, leaf_size
            )
            coef_sum = packed[:, clusters_here * leaf_size :].reshape(
                rhs_here, clusters_here, rank_size
            )
        with jax.named_scope("far_field"):
            far_field = jnp.einsum(
                "rck,ckl->rcl", coef_sum, row_f32, precision=lax.Precision.HIGH
            )
        if scaled is None:
            scaled = [coefficients[d] * source for d in range(degree_top)]
        result = near_sum + far_field + scaled[degree]
        iterate = result.astype(jnp.bfloat16)
    return result.reshape(rhs_here, clusters_here * leaf_size)


def solution(mesh):
    return jax.shard_map(
        shards,
        mesh=mesh,
        in_specs=(
            P("rhs", ("groups", "clus")),
            P(),
            P(("groups", "clus", "pair"), None, None),
            P(("groups", "clus", "pair")),
            P(("groups", "clus", "pair")),
            P(("groups", "clus"), None, None),
            P(("groups", "clus", "pair"), None, None),
            P(("groups", "clus", "pair")),
            P(("groups", "clus", "pair")),
        ),
        out_specs=P("rhs", ("groups", "clus")),
        check_vma=False,
    )
```

```python
import jax
import jax.numpy as jnp
from jax import lax
from jax.sharding import PartitionSpec as P


def shift(value, axis, count, step):
    return lax.ppermute(value, axis, [(i, (i + step) % count) for i in range(count)])


def pair_total(value, pair_count, pair_index):
    if pair_count == 1:
        return value
    if pair_count == 2:
        return value + shift(value, "pair", 2, 1)
    received = [value] + [shift(value, "pair", pair_count, s) for s in range(1, pair_count)]
    stacked = jnp.stack(received)
    order = (pair_index - jnp.arange(pair_count)) % pair_count
    canonical = stacked[order]
    total = canonical[0]
    for q in range(1, pair_count):
        total = total + canonical[q]
    return total


def shards(
    rhs_field, coefficients, near_blocks, near_tgt, near_src, row_basis, col_basis, far_src, far_tgt
):
    rhs_here = rhs_field.shape[0]
    clusters_here = row_basis.shape[0]
    rank_size = row_basis.shape[1]
    leaf_size = row_basis.shape[2]
    peer_count = lax.axis_size("clus")
    pair_count = lax.axis_size("pair")
    cluster_count = clusters_here * peer_count
    degree_top = coefficients.shape[0] - 1
    my_index = lax.axis_index("clus")
    pair_index = lax.axis_index("pair")
    my_base = my_index * clusters_here
    source = rhs_field.reshape(rhs_here, clusters_here, leaf_size)

    target_local = near_tgt - my_base
    target_hot = (target_local[:, None] == jnp.arange(clusters_here)[None, :]).astype(jnp.float32)
    relative = (near_src // clusters_here - my_index) % peer_count
    slot = jnp.where(relative == 0, 0, jnp.where(relative == 1, 1, 2))
    near_index = slot * clusters_here + near_src % clusters_here
    is_local = relative == 0
    local_index = jnp.where(is_local, near_src - my_base, 0)
    local_hot = target_hot * is_local[:, None].astype(jnp.float32)
    remote_count = min(4, near_tgt.shape[0]) if peer_count > 1 else 0
    remote_rows = jnp.argsort(is_local.astype(jnp.int32), stable=True)[:remote_count]
    remote_blocks = near_blocks[remote_rows]
    remote_index = near_index[remote_rows] - clusters_here
    remote_hot = target_hot[remote_rows]

    far_local = far_src - my_base
    far_hot = (far_tgt[:, None] == jnp.arange(cluster_count)[None, :]).astype(jnp.float32)
    row_f32 = row_basis.astype(jnp.float32)

    iterate = (coefficients[degree_top] * source).astype(jnp.bfloat16)
    result = source
    for step in range(degree_top):
        degree = degree_top - 1 - step
        with jax.named_scope("far_partial"):
            far_input = iterate[:, far_local, :]
            coef = jnp.einsum(
                "rjl,jkl->jrk", far_input, col_basis, preferred_element_type=jnp.float32
            )
            coef = coef.reshape(coef.shape[0], rhs_here * rank_size)
            partial_value = jnp.einsum("jc,jm->cm", far_hot, coef, precision=lax.Precision.HIGHEST)
            partial_value = partial_value.reshape(peer_count, clusters_here, rhs_here, rank_size)
            partial_value = partial_value.transpose(0, 2, 1, 3).reshape(
                peer_count, rhs_here, clusters_here * rank_size
            )
        with jax.named_scope("clus_exchange"):
            far_mine = partial_value[my_index]
            iterate_wide = iterate.reshape(rhs_here, clusters_here * leaf_size).astype(jnp.float32)
            iterate_size = clusters_here * leaf_size
            from_minus = iterate
            from_plus = iterate
            for s in range(1, peer_count):
                outgoing = partial_value[(my_index + s) % peer_count]
                carries_iterate = s == 1 or s == peer_count - 1
                if carries_iterate:
                    outgoing = jnp.concatenate([iterate_wide, outgoing], axis=1)
                incoming = shift(outgoing, "clus", peer_count, s)
                if carries_iterate:
                    neighbour = incoming[:, :iterate_size].astype(jnp.bfloat16)
                    neighbour = neighbour.reshape(rhs_here, clusters_here, leaf_size)
                    if s == 1:
                        from_minus = neighbour
                    if s == peer_count - 1:
                        from_plus = neighbour
                    incoming = incoming[:, iterate_size:]
                far_mine = far_mine + incoming
        with jax.named_scope("near_local"):
            gathered = iterate[:, local_index, :]
            contrib = jnp.einsum(
                "rjs,jts->rjt", gathered, near_blocks, preferred_element_type=jnp.float32
            )
            near_part = jnp.einsum(
                "rjt,jc->rct", contrib, local_hot, precision=lax.Precision.HIGHEST
            )
        with jax.named_scope("near_remote"):
            if remote_count:
                neighbours = jnp.concatenate([from_plus, from_minus], axis=1)
                gathered = neighbours[:, remote_index, :]
                contrib = jnp.einsum(
                    "rjs,jts->rjt", gathered, remote_blocks, preferred_element_type=jnp.float32
                )
                near_part = near_part + jnp.einsum(
                    "rjt,jc->rct", contrib, remote_hot, precision=lax.Precision.HIGHEST
                )
        with jax.named_scope("pair_sums"):
            near_flat = near_part.reshape(rhs_here, clusters_here * leaf_size)
            packed = jnp.concatenate([near_flat, far_mine], axis=1)
            packed = pair_total(packed, pair_count, pair_index)
            near_sum = packed[:, : clusters_here * leaf_size].reshape(
                rhs_here, clusters_here, leaf_size
            )
            coef_sum = packed[:, clusters_here * leaf_size :].reshape(
                rhs_here, clusters_here, rank_size
            )
        with jax.named_scope("far_field"):
            far_field = jnp.einsum(
                "rck,ckl->rcl", coef_sum, row_f32, precision=lax.Precision.HIGHEST
            )
        result = near_sum + far_field + coefficients[degree] * source
        iterate = result.astype(jnp.bfloat16)
    return result.reshape(rhs_here, clusters_here * leaf_size)


def solution(mesh):
    return jax.shard_map(
        shards,
        mesh=mesh,
        in_specs=(
            P("rhs", ("groups", "clus")),
            P(),
            P(("groups", "clus", "pair"), None, None),
            P(("groups", "clus", "pair")),
            P(("groups", "clus", "pair")),
            P(("groups", "clus"), None, None),
            P(("groups", "clus", "pair"), None, None),
            P(("groups", "clus", "pair")),
            P(("groups", "clus", "pair")),
        ),
        out_specs=P("rhs", ("groups", "clus")),
        check_vma=False,
    )
```

```python
import jax
import jax.numpy as jnp
from jax import lax
from jax.sharding import PartitionSpec as P


def shift(value, axis, count, step):
    return lax.ppermute(value, axis, [(i, (i + step) % count) for i in range(count)])


def pair_total(value, pair_count, pair_index):
    if pair_count == 1:
        return value
    if pair_count == 2:
        return value + shift(value, "pair", 2, 1)
    received = [value] + [shift(value, "pair", pair_count, s) for s in range(1, pair_count)]
    stacked = jnp.stack(received)
    order = (pair_index - jnp.arange(pair_count)) % pair_count
    canonical = stacked[order]
    total = canonical[0]
    for q in range(1, pair_count):
        total = total + canonical[q]
    return total


def shards(
    rhs_field, coefficients, near_blocks, near_tgt, near_src, row_basis, col_basis, far_src, far_tgt
):
    rhs_here = rhs_field.shape[0]
    clusters_here = row_basis.shape[0]
    rank_size = row_basis.shape[1]
    leaf_size = row_basis.shape[2]
    peer_count = lax.axis_size("clus")
    pair_count = lax.axis_size("pair")
    cluster_count = clusters_here * peer_count
    degree_top = coefficients.shape[0] - 1
    my_index = lax.axis_index("clus")
    pair_index = lax.axis_index("pair")
    my_base = my_index * clusters_here
    source = rhs_field.reshape(rhs_here, clusters_here, leaf_size)

    target_local = near_tgt - my_base
    target_hot = (target_local[:, None] == jnp.arange(clusters_here)[None, :]).astype(jnp.float32)
    relative = (near_src // clusters_here - my_index) % peer_count
    slot = jnp.where(relative == 0, 0, jnp.where(relative == 1, 1, 2))
    near_index = slot * clusters_here + near_src % clusters_here

    far_local = far_src - my_base
    far_hot = (far_tgt[:, None] == jnp.arange(cluster_count)[None, :]).astype(jnp.float32)
    row_f32 = row_basis.astype(jnp.float32)

    iterate = (coefficients[degree_top] * source).astype(jnp.bfloat16)
    result = source
    scaled = None
    for step in range(degree_top):
        degree = degree_top - 1 - step
        with jax.named_scope("far_partial"):
            far_input = iterate[:, far_local, :]
            coef = jnp.einsum(
                "rjl,jkl->jrk", far_input, col_basis, preferred_element_type=jnp.float32
            )
            coef = coef.reshape(coef.shape[0], rhs_here * rank_size)
            partial_value = jnp.einsum("jc,jm->cm", far_hot, coef, precision=lax.Precision.HIGHEST)
            partial_value = partial_value.reshape(peer_count, clusters_here, rhs_here, rank_size)
            partial_value = partial_value.transpose(0, 2, 1, 3).reshape(
                peer_count, rhs_here, clusters_here * rank_size
            )
        with jax.named_scope("clus_exchange"):
            far_mine = partial_value[my_index]
            iterate_wide = iterate.reshape(rhs_here, clusters_here * leaf_size).astype(jnp.float32)
            iterate_size = clusters_here * leaf_size
            from_minus = iterate
            from_plus = iterate
            for s in range(1, peer_count):
                outgoing = partial_value[(my_index + s) % peer_count]
                carries_iterate = s == 1 or s == peer_count - 1
                if carries_iterate:
                    outgoing = jnp.concatenate([iterate_wide, outgoing], axis=1)
                if scaled is None:
                    source_late, outgoing = lax.optimization_barrier((source, outgoing))
                    scaled = [coefficients[d] * source_late for d in range(degree_top)]
                incoming = shift(outgoing, "clus", peer_count, s)
                if carries_iterate:
                    neighbour = incoming[:, :iterate_size].astype(jnp.bfloat16)
                    neighbour = neighbour.reshape(rhs_here, clusters_here, leaf_size)
                    if s == 1:
                        from_minus = neighbour
                    if s == peer_count - 1:
                        from_plus = neighbour
                    incoming = incoming[:, iterate_size:]
                far_mine = far_mine + incoming
        with jax.named_scope("near_partial"):
            extended = jnp.concatenate([iterate, from_plus, from_minus], axis=1)
            gathered = extended[:, near_index, :]
            contrib = jnp.einsum(
                "rjs,jts->rjt", gathered, near_blocks, preferred_element_type=jnp.float32
            )
            near_part = jnp.einsum(
                "rjt,jc->rct", contrib, target_hot, precision=lax.Precision.HIGHEST
            )
        with jax.named_scope("pair_sums"):
            near_flat = near_part.reshape(rhs_here, clusters_here * leaf_size)
            packed = jnp.concatenate([near_flat, far_mine], axis=1)
            packed = pair_total(packed, pair_count, pair_index)
            near_sum = packed[:, : clusters_here * leaf_size].reshape(
                rhs_here, clusters_here, leaf_size
            )
            coef_sum = packed[:, clusters_here * leaf_size :].reshape(
                rhs_here, clusters_here, rank_size
            )
        with jax.named_scope("far_field"):
            far_field = jnp.einsum(
                "rck,ckl->rcl", coef_sum, row_f32, precision=lax.Precision.HIGHEST
            )
        if scaled is None:
            scaled = [coefficients[d] * source for d in range(degree_top)]
        result = near_sum + far_field + scaled[degree]
        iterate = result.astype(jnp.bfloat16)
    return result.reshape(rhs_here, clusters_here * leaf_size)


def solution(mesh):
    return jax.shard_map(
        shards,
        mesh=mesh,
        in_specs=(
            P("rhs", ("groups", "clus")),
            P(),
            P(("groups", "clus", "pair"), None, None),
            P(("groups", "clus", "pair")),
            P(("groups", "clus", "pair")),
            P(("groups", "clus"), None, None),
            P(("groups", "clus", "pair"), None, None),
            P(("groups", "clus", "pair")),
            P(("groups", "clus", "pair")),
        ),
        out_specs=P("rhs", ("groups", "clus")),
        check_vma=False,
    )
```

```python
import jax
import jax.numpy as jnp
from jax import lax
from jax.sharding import PartitionSpec as P


def shift(value, axis, count, step):
    return lax.ppermute(value, axis, [(i, (i + step) % count) for i in range(count)])


def split_three(value):
    high = lax.reduce_precision(value, exponent_bits=8, mantissa_bits=7)
    rest = value - high
    middle = lax.reduce_precision(rest, exponent_bits=8, mantissa_bits=7)
    low = rest - middle
    parts = [high, middle, low]
    return jnp.concatenate([part.astype(jnp.bfloat16) for part in parts], axis=-1)


def join_three(parts):
    width = parts.shape[-1] // 3
    high, middle, low = (
        parts[..., k * width : (k + 1) * width].astype(jnp.float32) for k in range(3)
    )
    return (high + middle) + low


def pair_total(value, pair_count, pair_index):
    if pair_count == 1:
        return value
    if pair_count == 2:
        return value + shift(value, "pair", 2, 1)
    received = [value] + [shift(value, "pair", pair_count, s) for s in range(1, pair_count)]
    stacked = jnp.stack(received)
    order = (pair_index - jnp.arange(pair_count)) % pair_count
    canonical = stacked[order]
    total = canonical[0]
    for q in range(1, pair_count):
        total = total + canonical[q]
    return total


def shards(
    rhs_field, coefficients, near_blocks, near_tgt, near_src, row_basis, col_basis, far_src, far_tgt
):
    rhs_here = rhs_field.shape[0]
    clusters_here = row_basis.shape[0]
    rank_size = row_basis.shape[1]
    leaf_size = row_basis.shape[2]
    peer_count = lax.axis_size("clus")
    pair_count = lax.axis_size("pair")
    cluster_count = clusters_here * peer_count
    degree_top = coefficients.shape[0] - 1
    my_index = lax.axis_index("clus")
    pair_index = lax.axis_index("pair")
    my_base = my_index * clusters_here
    source = rhs_field.reshape(rhs_here, clusters_here, leaf_size)

    target_local = near_tgt - my_base
    target_hot = (target_local[:, None] == jnp.arange(clusters_here)[None, :]).astype(jnp.float32)
    relative = (near_src // clusters_here - my_index) % peer_count
    slot = jnp.where(relative == 0, 0, jnp.where(relative == 1, 1, 2))
    near_index = slot * clusters_here + near_src % clusters_here

    far_local = far_src - my_base
    far_hot = (far_tgt[:, None] == jnp.arange(cluster_count)[None, :]).astype(jnp.float32)
    row_f32 = row_basis.astype(jnp.float32)

    iterate = (coefficients[degree_top] * source).astype(jnp.bfloat16)
    result = source
    for step in range(degree_top):
        degree = degree_top - 1 - step
        with jax.named_scope("far_partial"):
            far_input = iterate[:, far_local, :]
            coef = jnp.einsum(
                "rjl,jkl->jrk", far_input, col_basis, preferred_element_type=jnp.float32
            )
            coef = coef.reshape(coef.shape[0], rhs_here * rank_size)
            partial_value = jnp.einsum("jc,jm->cm", far_hot, coef, precision=lax.Precision.HIGHEST)
            partial_value = partial_value.reshape(peer_count, clusters_here, rhs_here, rank_size)
            partial_value = partial_value.transpose(0, 2, 1, 3).reshape(
                peer_count, rhs_here, clusters_here * rank_size
            )
        with jax.named_scope("clus_exchange"):
            far_mine = partial_value[my_index]
            iterate_flat = iterate.reshape(rhs_here, clusters_here * leaf_size)
            iterate_size = clusters_here * leaf_size
            from_minus = iterate
            from_plus = iterate
            for s in range(1, peer_count):
                outgoing = split_three(partial_value[(my_index + s) % peer_count])
                carries_iterate = s == 1 or s == peer_count - 1
                if carries_iterate:
                    outgoing = jnp.concatenate([iterate_flat, outgoing], axis=1)
                incoming = shift(outgoing, "clus", peer_count, s)
                if carries_iterate:
                    neighbour = incoming[:, :iterate_size]
                    neighbour = neighbour.reshape(rhs_here, clusters_here, leaf_size)
                    if s == 1:
                        from_minus = neighbour
                    if s == peer_count - 1:
                        from_plus = neighbour
                    incoming = incoming[:, iterate_size:]
                far_mine = far_mine + join_three(incoming)
        with jax.named_scope("near_partial"):
            extended = jnp.concatenate([iterate, from_plus, from_minus], axis=1)
            gathered = extended[:, near_index, :]
            contrib = jnp.einsum(
                "rjs,jts->rjt", gathered, near_blocks, preferred_element_type=jnp.float32
            )
            near_part = jnp.einsum(
                "rjt,jc->rct", contrib, target_hot, precision=lax.Precision.HIGHEST
            )
        with jax.named_scope("pair_sums"):
            near_flat = near_part.reshape(rhs_here, clusters_here * leaf_size)
            packed = jnp.concatenate([near_flat, far_mine], axis=1)
            packed = pair_total(packed, pair_count, pair_index)
            near_sum = packed[:, : clusters_here * leaf_size].reshape(
                rhs_here, clusters_here, leaf_size
            )
            coef_sum = packed[:, clusters_here * leaf_size :].reshape(
                rhs_here, clusters_here, rank_size
            )
        with jax.named_scope("far_field"):
            far_field = jnp.einsum(
                "rck,ckl->rcl", coef_sum, row_f32, precision=lax.Precision.HIGHEST
            )
        result = near_sum + far_field + coefficients[degree] * source
        iterate = result.astype(jnp.bfloat16)
    return result.reshape(rhs_here, clusters_here * leaf_size)


def solution(mesh):
    return jax.shard_map(
        shards,
        mesh=mesh,
        in_specs=(
            P("rhs", ("groups", "clus")),
            P(),
            P(("groups", "clus", "pair"), None, None),
            P(("groups", "clus", "pair")),
            P(("groups", "clus", "pair")),
            P(("groups", "clus"), None, None),
            P(("groups", "clus", "pair"), None, None),
            P(("groups", "clus", "pair")),
            P(("groups", "clus", "pair")),
        ),
        out_specs=P("rhs", ("groups", "clus")),
        check_vma=False,
    )
```

```python
import jax
import jax.numpy as jnp
from jax import lax
from jax.sharding import PartitionSpec as P


def shift(value, axis, count, step):
    return lax.ppermute(value, axis, [(i, (i + step) % count) for i in range(count)])


def split_three(value):
    high = lax.reduce_precision(value, exponent_bits=8, mantissa_bits=7)
    rest = value - high
    middle = lax.reduce_precision(rest, exponent_bits=8, mantissa_bits=7)
    low = rest - middle
    parts = [high, middle, low]
    return jnp.concatenate([part.astype(jnp.bfloat16) for part in parts], axis=-1)


def join_three(parts):
    width = parts.shape[-1] // 3
    high, middle, low = (
        parts[..., k * width : (k + 1) * width].astype(jnp.float32) for k in range(3)
    )
    return (high + middle) + low


def pair_total(value, pair_count, pair_index):
    if pair_count == 1:
        return value
    if pair_count == 2:
        return value + shift(value, "pair", 2, 1)
    received = [value] + [shift(value, "pair", pair_count, s) for s in range(1, pair_count)]
    stacked = jnp.stack(received)
    order = (pair_index - jnp.arange(pair_count)) % pair_count
    canonical = stacked[order]
    total = canonical[0]
    for q in range(1, pair_count):
        total = total + canonical[q]
    return total


def shards(
    rhs_field, coefficients, near_blocks, near_tgt, near_src, row_basis, col_basis, far_src, far_tgt
):
    rhs_here = rhs_field.shape[0]
    clusters_here = row_basis.shape[0]
    rank_size = row_basis.shape[1]
    leaf_size = row_basis.shape[2]
    peer_count = lax.axis_size("clus")
    pair_count = lax.axis_size("pair")
    cluster_count = clusters_here * peer_count
    degree_top = coefficients.shape[0] - 1
    my_index = lax.axis_index("clus")
    pair_index = lax.axis_index("pair")
    my_base = my_index * clusters_here
    source = rhs_field.reshape(rhs_here, clusters_here, leaf_size).transpose(1, 0, 2)

    target_local = near_tgt - my_base
    target_hot = (target_local[:, None] == jnp.arange(clusters_here)[None, :]).astype(jnp.float32)
    relative = (near_src // clusters_here - my_index) % peer_count
    slot = jnp.where(relative == 0, 0, jnp.where(relative == 1, 1, 2))
    near_index = slot * clusters_here + near_src % clusters_here

    far_local = far_src - my_base
    far_hot = (far_tgt[:, None] == jnp.arange(cluster_count)[None, :]).astype(jnp.float32)
    row_f32 = row_basis.astype(jnp.float32)
    iterate_size = rhs_here * leaf_size
    coef_size = rhs_here * rank_size

    iterate = (coefficients[degree_top] * source).astype(jnp.bfloat16)
    result = source
    for step in range(degree_top):
        degree = degree_top - 1 - step
        with jax.named_scope("far_partial"):
            far_input = iterate[far_local]
            coef = jnp.einsum(
                "jrl,jkl->jrk", far_input, col_basis, preferred_element_type=jnp.float32
            )
            coef = coef.reshape(coef.shape[0], coef_size)
            partial_value = jnp.einsum("jc,jm->cm", far_hot, coef, precision=lax.Precision.HIGHEST)
            partial_value = partial_value.reshape(peer_count, clusters_here, coef_size)
        with jax.named_scope("clus_exchange"):
            far_mine = partial_value[my_index]
            iterate_flat = iterate.reshape(clusters_here, iterate_size)
            from_minus = iterate
            from_plus = iterate
            for s in range(1, peer_count):
                outgoing = split_three(partial_value[(my_index + s) % peer_count])
                carries_iterate = s == 1 or s == peer_count - 1
                if carries_iterate:
                    outgoing = jnp.concatenate([iterate_flat, outgoing], axis=1)
                incoming = shift(outgoing, "clus", peer_count, s)
                if carries_iterate:
                    neighbour = incoming[:, :iterate_size]
                    neighbour = neighbour.reshape(clusters_here, rhs_here, leaf_size)
                    if s == 1:
                        from_minus = neighbour
                    if s == peer_count - 1:
                        from_plus = neighbour
                    incoming = incoming[:, iterate_size:]
                far_mine = far_mine + join_three(incoming)
        with jax.named_scope("near_partial"):
            extended = jnp.concatenate([iterate, from_plus, from_minus], axis=0)
            gathered = extended[near_index]
            contrib = jnp.einsum(
                "jrs,jts->jrt", gathered, near_blocks, preferred_element_type=jnp.float32
            )
            contrib = contrib.reshape(contrib.shape[0], iterate_size)
            near_part = jnp.einsum(
                "jc,jm->cm", target_hot, contrib, precision=lax.Precision.HIGHEST
            )
        with jax.named_scope("pair_sums"):
            packed = jnp.concatenate([near_part, far_mine], axis=1)
            packed = pair_total(packed, pair_count, pair_index)
            near_sum = packed[:, :iterate_size].reshape(clusters_here, rhs_here, leaf_size)
            coef_sum = packed[:, iterate_size:].reshape(clusters_here, rhs_here, rank_size)
        with jax.named_scope("far_field"):
            far_field = jnp.einsum(
                "crk,ckl->crl", coef_sum, row_f32, precision=lax.Precision.HIGHEST
            )
        result = near_sum + far_field + coefficients[degree] * source
        iterate = result.astype(jnp.bfloat16)
    return result.transpose(1, 0, 2).reshape(rhs_here, clusters_here * leaf_size)


def solution(mesh):
    return jax.shard_map(
        shards,
        mesh=mesh,
        in_specs=(
            P("rhs", ("groups", "clus")),
            P(),
            P(("groups", "clus", "pair"), None, None),
            P(("groups", "clus", "pair")),
            P(("groups", "clus", "pair")),
            P(("groups", "clus"), None, None),
            P(("groups", "clus", "pair"), None, None),
            P(("groups", "clus", "pair")),
            P(("groups", "clus", "pair")),
        ),
        out_specs=P("rhs", ("groups", "clus")),
        check_vma=False,
    )
```

```python
import jax
import jax.numpy as jnp
from jax import lax
from jax.sharding import PartitionSpec as P


def shift(value, axis, count, step):
    return lax.ppermute(value, axis, [(i, (i + step) % count) for i in range(count)])


def split_three(value):
    high = lax.reduce_precision(value, exponent_bits=8, mantissa_bits=7)
    rest = value - high
    middle = lax.reduce_precision(rest, exponent_bits=8, mantissa_bits=7)
    low = rest - middle
    parts = [high, middle, low]
    return jnp.concatenate([part.astype(jnp.bfloat16) for part in parts], axis=-1)


def join_three(parts):
    width = parts.shape[-1] // 3
    high, middle, low = (
        parts[..., k * width : (k + 1) * width].astype(jnp.float32) for k in range(3)
    )
    return (high + middle) + low


def pair_total(value, pair_count, pair_index):
    if pair_count == 1:
        return value
    if pair_count == 2:
        return value + shift(value, "pair", 2, 1)
    received = [value] + [shift(value, "pair", pair_count, s) for s in range(1, pair_count)]
    stacked = jnp.stack(received)
    order = (pair_index - jnp.arange(pair_count)) % pair_count
    canonical = stacked[order]
    total = canonical[0]
    for q in range(1, pair_count):
        total = total + canonical[q]
    return total


def shards(
    rhs_field, coefficients, near_blocks, near_tgt, near_src, row_basis, col_basis, far_src, far_tgt
):
    rhs_here = rhs_field.shape[0]
    clusters_here = row_basis.shape[0]
    rank_size = row_basis.shape[1]
    leaf_size = row_basis.shape[2]
    peer_count = lax.axis_size("clus")
    pair_count = lax.axis_size("pair")
    cluster_count = clusters_here * peer_count
    degree_top = coefficients.shape[0] - 1
    my_index = lax.axis_index("clus")
    pair_index = lax.axis_index("pair")
    my_base = my_index * clusters_here
    source = rhs_field.reshape(rhs_here, clusters_here, leaf_size).transpose(1, 0, 2)

    target_local = near_tgt - my_base
    target_hot = (target_local[:, None] == jnp.arange(clusters_here)[None, :]).astype(jnp.float32)
    relative = (near_src // clusters_here - my_index) % peer_count
    slot = jnp.where(relative == 0, 0, jnp.where(relative == 1, 1, 2))
    near_index = slot * clusters_here + near_src % clusters_here
    near_pick = (near_index[:, None] == jnp.arange(3 * clusters_here)[None, :]).astype(jnp.bfloat16)

    far_local = far_src - my_base
    far_hot = (far_tgt[:, None] == jnp.arange(cluster_count)[None, :]).astype(jnp.float32)
    far_pick = (far_local[:, None] == jnp.arange(clusters_here)[None, :]).astype(jnp.bfloat16)
    row_f32 = row_basis.astype(jnp.float32)
    iterate_size = rhs_here * leaf_size
    coef_size = rhs_here * rank_size

    iterate = (coefficients[degree_top] * source).astype(jnp.bfloat16)
    result = source
    for step in range(degree_top):
        degree = degree_top - 1 - step
        with jax.named_scope("far_partial"):
            far_input = jnp.einsum(
                "jc,cm->jm",
                far_pick,
                iterate.reshape(clusters_here, iterate_size),
                preferred_element_type=jnp.bfloat16,
            ).reshape(far_pick.shape[0], rhs_here, leaf_size)
            coef = jnp.einsum(
                "jrl,jkl->jrk", far_input, col_basis, preferred_element_type=jnp.float32
            )
            coef = coef.reshape(coef.shape[0], coef_size)
            partial_value = jnp.einsum("jc,jm->cm", far_hot, coef, precision=lax.Precision.HIGHEST)
            partial_value = partial_value.reshape(peer_count, clusters_here, coef_size)
        with jax.named_scope("clus_exchange"):
            far_mine = partial_value[my_index]
            iterate_flat = iterate.reshape(clusters_here, iterate_size)
            from_minus = iterate
            from_plus = iterate
            for s in range(1, peer_count):
                outgoing = split_three(partial_value[(my_index + s) % peer_count])
                carries_iterate = s == 1 or s == peer_count - 1
                if carries_iterate:
                    outgoing = jnp.concatenate([iterate_flat, outgoing], axis=1)
                incoming = shift(outgoing, "clus", peer_count, s)
                if carries_iterate:
                    neighbour = incoming[:, :iterate_size]
                    neighbour = neighbour.reshape(clusters_here, rhs_here, leaf_size)
                    if s == 1:
                        from_minus = neighbour
                    if s == peer_count - 1:
                        from_plus = neighbour
                    incoming = incoming[:, iterate_size:]
                far_mine = far_mine + join_three(incoming)
        with jax.named_scope("near_partial"):
            extended = jnp.concatenate([iterate, from_plus, from_minus], axis=0)
            gathered = jnp.einsum(
                "jc,cm->jm",
                near_pick,
                extended.reshape(3 * clusters_here, iterate_size),
                preferred_element_type=jnp.bfloat16,
            ).reshape(near_pick.shape[0], rhs_here, leaf_size)
            contrib = jnp.einsum(
                "jrs,jts->jrt", gathered, near_blocks, preferred_element_type=jnp.float32
            )
            contrib = contrib.reshape(contrib.shape[0], iterate_size)
            near_part = jnp.einsum(
                "jc,jm->cm", target_hot, contrib, precision=lax.Precision.HIGHEST
            )
        with jax.named_scope("pair_sums"):
            packed = jnp.concatenate([near_part, far_mine], axis=1)
            packed = pair_total(packed, pair_count, pair_index)
            near_sum = packed[:, :iterate_size].reshape(clusters_here, rhs_here, leaf_size)
            coef_sum = packed[:, iterate_size:].reshape(clusters_here, rhs_here, rank_size)
        with jax.named_scope("far_field"):
            far_field = jnp.einsum(
                "crk,ckl->crl", coef_sum, row_f32, precision=lax.Precision.HIGHEST
            )
        result = near_sum + far_field + coefficients[degree] * source
        iterate = result.astype(jnp.bfloat16)
    return result.transpose(1, 0, 2).reshape(rhs_here, clusters_here * leaf_size)


def solution(mesh):
    return jax.shard_map(
        shards,
        mesh=mesh,
        in_specs=(
            P("rhs", ("groups", "clus")),
            P(),
            P(("groups", "clus", "pair"), None, None),
            P(("groups", "clus", "pair")),
            P(("groups", "clus", "pair")),
            P(("groups", "clus"), None, None),
            P(("groups", "clus", "pair"), None, None),
            P(("groups", "clus", "pair")),
            P(("groups", "clus", "pair")),
        ),
        out_specs=P("rhs", ("groups", "clus")),
        check_vma=False,
    )
```

```python
import jax
import jax.numpy as jnp
from jax import lax
from jax.sharding import PartitionSpec as P


def shift(value, axis, count, step):
    return lax.ppermute(value, axis, [(i, (i + step) % count) for i in range(count)])


def split_three(value):
    high = lax.reduce_precision(value, exponent_bits=8, mantissa_bits=7)
    rest = value - high
    middle = lax.reduce_precision(rest, exponent_bits=8, mantissa_bits=7)
    low = rest - middle
    parts = [high, middle, low]
    return jnp.concatenate([part.astype(jnp.bfloat16) for part in parts], axis=-1)


def join_three(parts):
    width = parts.shape[-1] // 3
    high, middle, low = (
        parts[..., k * width : (k + 1) * width].astype(jnp.float32) for k in range(3)
    )
    return (high + middle) + low


def pair_total(value, pair_count, pair_index):
    if pair_count == 1:
        return value
    if pair_count == 2:
        return value + shift(value, "pair", 2, 1)
    received = [value] + [shift(value, "pair", pair_count, s) for s in range(1, pair_count)]
    stacked = jnp.stack(received)
    order = (pair_index - jnp.arange(pair_count)) % pair_count
    canonical = stacked[order]
    total = canonical[0]
    for q in range(1, pair_count):
        total = total + canonical[q]
    return total


def shards(
    rhs_field, coefficients, near_blocks, near_tgt, near_src, row_basis, col_basis, far_src, far_tgt
):
    rhs_here = rhs_field.shape[0]
    clusters_here = row_basis.shape[0]
    rank_size = row_basis.shape[1]
    leaf_size = row_basis.shape[2]
    peer_count = lax.axis_size("clus")
    pair_count = lax.axis_size("pair")
    cluster_count = clusters_here * peer_count
    degree_top = coefficients.shape[0] - 1
    my_index = lax.axis_index("clus")
    pair_index = lax.axis_index("pair")
    my_base = my_index * clusters_here
    source = rhs_field.reshape(rhs_here, clusters_here, leaf_size).transpose(1, 0, 2)

    target_local = near_tgt - my_base
    target_hot = (target_local[:, None] == jnp.arange(clusters_here)[None, :]).astype(jnp.float32)
    relative = (near_src // clusters_here - my_index) % peer_count
    slot = jnp.where(relative == 0, 0, jnp.where(relative == 1, 1, 2))
    near_index = slot * clusters_here + near_src % clusters_here
    near_pick = (near_index[:, None] == jnp.arange(3 * clusters_here)[None, :]).astype(jnp.bfloat16)

    far_local = far_src - my_base
    far_hot = (far_tgt[:, None] == jnp.arange(cluster_count)[None, :]).astype(jnp.float32)
    far_pick = (far_local[:, None] == jnp.arange(clusters_here)[None, :]).astype(jnp.bfloat16)
    row_f32 = row_basis.astype(jnp.float32)
    iterate_size = rhs_here * leaf_size
    coef_size = rhs_here * rank_size

    iterate = (coefficients[degree_top] * source).astype(jnp.bfloat16)
    result = source
    for step in range(degree_top):
        degree = degree_top - 1 - step
        with jax.named_scope("far_partial"):
            far_input = jnp.einsum(
                "jc,cm->jm",
                far_pick,
                iterate.reshape(clusters_here, iterate_size),
                preferred_element_type=jnp.bfloat16,
            ).reshape(far_pick.shape[0], rhs_here, leaf_size)
            coef = jnp.einsum(
                "jrl,jkl->jrk", far_input, col_basis, preferred_element_type=jnp.float32
            )
            coef = coef.reshape(coef.shape[0], coef_size)
            partial_value = jnp.einsum("jc,jm->cm", far_hot, coef, precision=lax.Precision.HIGHEST)
            partial_value = partial_value.reshape(peer_count, clusters_here, coef_size)
        with jax.named_scope("clus_exchange"):
            far_mine = partial_value[my_index]
            iterate_flat = iterate.reshape(clusters_here, iterate_size)
            from_minus = iterate
            from_plus = iterate
            for s in range(1, peer_count):
                outgoing = split_three(partial_value[(my_index + s) % peer_count])
                carries_iterate = s == 1 or s == peer_count - 1
                if carries_iterate:
                    outgoing = jnp.concatenate([iterate_flat, outgoing], axis=1)
                incoming = shift(outgoing, "clus", peer_count, s)
                if carries_iterate:
                    neighbour = incoming[:, :iterate_size]
                    neighbour = neighbour.reshape(clusters_here, rhs_here, leaf_size)
                    if s == 1:
                        from_minus = neighbour
                    if s == peer_count - 1:
                        from_plus = neighbour
                    incoming = incoming[:, iterate_size:]
                far_mine = far_mine + join_three(incoming)
        with jax.named_scope("near_partial"):
            extended = jnp.concatenate([iterate, from_plus, from_minus], axis=0)
            gathered = jnp.einsum(
                "jc,cm->jm",
                near_pick,
                extended.reshape(3 * clusters_here, iterate_size),
                preferred_element_type=jnp.bfloat16,
            ).reshape(near_pick.shape[0], rhs_here, leaf_size)
            contrib = jnp.einsum(
                "jrs,jts->jrt", gathered, near_blocks, preferred_element_type=jnp.float32
            )
            contrib = contrib.reshape(contrib.shape[0], iterate_size)
            near_part = jnp.einsum(
                "jc,jm->cm", target_hot, contrib, precision=lax.Precision.HIGHEST
            )
        with jax.named_scope("pair_sums"):
            packed = jnp.concatenate([near_part, far_mine], axis=1)
            packed = pair_total(packed, pair_count, pair_index)
            near_sum = packed[:, :iterate_size].reshape(clusters_here, rhs_here, leaf_size)
            coef_sum = packed[:, iterate_size:].reshape(clusters_here, rhs_here, rank_size)
        with jax.named_scope("far_field"):
            far_field = jnp.einsum(
                "crk,ckl->crl", coef_sum, row_f32, precision=lax.Precision.HIGHEST
            )
        scale, near_sum = lax.optimization_barrier((coefficients[degree], near_sum))
        result = near_sum + far_field + scale * source
        iterate = result.astype(jnp.bfloat16)
    return result.transpose(1, 0, 2).reshape(rhs_here, clusters_here * leaf_size)


def solution(mesh):
    return jax.shard_map(
        shards,
        mesh=mesh,
        in_specs=(
            P("rhs", ("groups", "clus")),
            P(),
            P(("groups", "clus", "pair"), None, None),
            P(("groups", "clus", "pair")),
            P(("groups", "clus", "pair")),
            P(("groups", "clus"), None, None),
            P(("groups", "clus", "pair"), None, None),
            P(("groups", "clus", "pair")),
            P(("groups", "clus", "pair")),
        ),
        out_specs=P("rhs", ("groups", "clus")),
        check_vma=False,
    )
```

```python
import jax
import jax.numpy as jnp
from jax import lax
from jax.sharding import PartitionSpec as P


def shift(value, axis, count, step):
    return lax.ppermute(value, axis, [(i, (i + step) % count) for i in range(count)])


def split_three(value):
    high = lax.reduce_precision(value, exponent_bits=8, mantissa_bits=7)
    rest = value - high
    middle = lax.reduce_precision(rest, exponent_bits=8, mantissa_bits=7)
    low = rest - middle
    parts = [high, middle, low]
    return jnp.concatenate([part.astype(jnp.bfloat16) for part in parts], axis=-1)


def join_three(parts):
    width = parts.shape[-1] // 3
    high, middle, low = (
        parts[..., k * width : (k + 1) * width].astype(jnp.float32) for k in range(3)
    )
    return (high + middle) + low


def pair_total(value, pair_count, pair_index):
    if pair_count == 1:
        return value
    if pair_count == 2:
        return value + shift(value, "pair", 2, 1)
    received = [value] + [shift(value, "pair", pair_count, s) for s in range(1, pair_count)]
    stacked = jnp.stack(received)
    order = (pair_index - jnp.arange(pair_count)) % pair_count
    canonical = stacked[order]
    total = canonical[0]
    for q in range(1, pair_count):
        total = total + canonical[q]
    return total


def shards(
    rhs_field, coefficients, near_blocks, near_tgt, near_src, row_basis, col_basis, far_src, far_tgt
):
    rhs_here = rhs_field.shape[0]
    clusters_here = row_basis.shape[0]
    rank_size = row_basis.shape[1]
    leaf_size = row_basis.shape[2]
    peer_count = lax.axis_size("clus")
    pair_count = lax.axis_size("pair")
    cluster_count = clusters_here * peer_count
    degree_top = coefficients.shape[0] - 1
    my_index = lax.axis_index("clus")
    pair_index = lax.axis_index("pair")
    my_base = my_index * clusters_here
    source = rhs_field.reshape(rhs_here, clusters_here, leaf_size).transpose(1, 0, 2)

    target_local = near_tgt - my_base
    target_hot = (target_local[:, None] == jnp.arange(clusters_here)[None, :]).astype(jnp.float32)
    relative = (near_src // clusters_here - my_index) % peer_count
    slot = jnp.where(relative == 0, 0, jnp.where(relative == 1, 1, 2))
    near_index = slot * clusters_here + near_src % clusters_here
    near_pick = (near_index[:, None] == jnp.arange(3 * clusters_here)[None, :]).astype(jnp.bfloat16)

    far_local = far_src - my_base
    far_hot = (far_tgt[:, None] == jnp.arange(cluster_count)[None, :]).astype(jnp.float32)
    far_pick = (far_local[:, None] == jnp.arange(clusters_here)[None, :]).astype(jnp.bfloat16)
    row_f32 = row_basis.astype(jnp.float32)
    iterate_size = rhs_here * leaf_size
    coef_size = rhs_here * rank_size

    iterate = (coefficients[degree_top] * source).astype(jnp.bfloat16)
    result = source
    scaled = None
    for step in range(degree_top):
        degree = degree_top - 1 - step
        with jax.named_scope("far_partial"):
            far_input = jnp.einsum(
                "jc,cm->jm",
                far_pick,
                iterate.reshape(clusters_here, iterate_size),
                preferred_element_type=jnp.bfloat16,
            ).reshape(far_pick.shape[0], rhs_here, leaf_size)
            coef = jnp.einsum(
                "jrl,jkl->jrk", far_input, col_basis, preferred_element_type=jnp.float32
            )
            coef = coef.reshape(coef.shape[0], coef_size)
            partial_value = jnp.einsum("jc,jm->cm", far_hot, coef, precision=lax.Precision.HIGHEST)
            partial_value = partial_value.reshape(peer_count, clusters_here, coef_size)
        with jax.named_scope("clus_exchange"):
            far_mine = partial_value[my_index]
            iterate_flat = iterate.reshape(clusters_here, iterate_size)
            from_minus = iterate
            from_plus = iterate
            for s in range(1, peer_count):
                outgoing = split_three(partial_value[(my_index + s) % peer_count])
                carries_iterate = s == 1 or s == peer_count - 1
                if carries_iterate:
                    outgoing = jnp.concatenate([iterate_flat, outgoing], axis=1)
                if s == 1 and scaled is None:
                    scales, outgoing = lax.optimization_barrier((coefficients, outgoing))
                    scaled = [scales[d] * source for d in range(degree_top)]
                incoming = shift(outgoing, "clus", peer_count, s)
                if carries_iterate:
                    neighbour = incoming[:, :iterate_size]
                    neighbour = neighbour.reshape(clusters_here, rhs_here, leaf_size)
                    if s == 1:
                        from_minus = neighbour
                    if s == peer_count - 1:
                        from_plus = neighbour
                    incoming = incoming[:, iterate_size:]
                far_mine = far_mine + join_three(incoming)
        with jax.named_scope("near_partial"):
            extended = jnp.concatenate([iterate, from_plus, from_minus], axis=0)
            gathered = jnp.einsum(
                "jc,cm->jm",
                near_pick,
                extended.reshape(3 * clusters_here, iterate_size),
                preferred_element_type=jnp.bfloat16,
            ).reshape(near_pick.shape[0], rhs_here, leaf_size)
            contrib = jnp.einsum(
                "jrs,jts->jrt", gathered, near_blocks, preferred_element_type=jnp.float32
            )
            contrib = contrib.reshape(contrib.shape[0], iterate_size)
            near_part = jnp.einsum(
                "jc,jm->cm", target_hot, contrib, precision=lax.Precision.HIGHEST
            )
        with jax.named_scope("pair_sums"):
            if scaled is None:
                scaled = [coefficients[d] * source for d in range(degree_top)]
            if step == 0:
                scaled, near_part = lax.optimization_barrier((scaled, near_part))
            packed = jnp.concatenate([near_part, far_mine], axis=1)
            packed = pair_total(packed, pair_count, pair_index)
            near_sum = packed[:, :iterate_size].reshape(clusters_here, rhs_here, leaf_size)
            coef_sum = packed[:, iterate_size:].reshape(clusters_here, rhs_here, rank_size)
        with jax.named_scope("far_field"):
            far_field = jnp.einsum(
                "crk,ckl->crl", coef_sum, row_f32, precision=lax.Precision.HIGHEST
            )
        result = near_sum + far_field + scaled[degree]
        iterate = result.astype(jnp.bfloat16)
    return result.transpose(1, 0, 2).reshape(rhs_here, clusters_here * leaf_size)


def solution(mesh):
    return jax.shard_map(
        shards,
        mesh=mesh,
        in_specs=(
            P("rhs", ("groups", "clus")),
            P(),
            P(("groups", "clus", "pair"), None, None),
            P(("groups", "clus", "pair")),
            P(("groups", "clus", "pair")),
            P(("groups", "clus"), None, None),
            P(("groups", "clus", "pair"), None, None),
            P(("groups", "clus", "pair")),
            P(("groups", "clus", "pair")),
        ),
        out_specs=P("rhs", ("groups", "clus")),
        check_vma=False,
    )
```

```python
import jax
import jax.numpy as jnp
from jax import lax
from jax.sharding import PartitionSpec as P


def shift(value, axis, count, step):
    return lax.ppermute(value, axis, [(i, (i + step) % count) for i in range(count)])


def split_three(value):
    high = lax.reduce_precision(value, exponent_bits=8, mantissa_bits=7)
    rest = value - high
    middle = lax.reduce_precision(rest, exponent_bits=8, mantissa_bits=7)
    low = rest - middle
    parts = [high, middle, low]
    return jnp.concatenate([part.astype(jnp.bfloat16) for part in parts], axis=-1)


def join_three(parts):
    width = parts.shape[-1] // 3
    high, middle, low = (
        parts[..., k * width : (k + 1) * width].astype(jnp.float32) for k in range(3)
    )
    return (high + middle) + low


def pair_total(value, pair_count, pair_index):
    if pair_count == 1:
        return value
    if pair_count == 2:
        return value + shift(value, "pair", 2, 1)
    received = [value] + [shift(value, "pair", pair_count, s) for s in range(1, pair_count)]
    stacked = jnp.stack(received)
    order = (pair_index - jnp.arange(pair_count)) % pair_count
    canonical = stacked[order]
    total = canonical[0]
    for q in range(1, pair_count):
        total = total + canonical[q]
    return total


def shards(
    rhs_field, coefficients, near_blocks, near_tgt, near_src, row_basis, col_basis, far_src, far_tgt
):
    rhs_here = rhs_field.shape[0]
    clusters_here = row_basis.shape[0]
    rank_size = row_basis.shape[1]
    leaf_size = row_basis.shape[2]
    peer_count = lax.axis_size("clus")
    pair_count = lax.axis_size("pair")
    cluster_count = clusters_here * peer_count
    degree_top = coefficients.shape[0] - 1
    my_index = lax.axis_index("clus")
    pair_index = lax.axis_index("pair")
    my_base = my_index * clusters_here
    source = rhs_field.reshape(rhs_here, clusters_here, leaf_size).transpose(1, 0, 2)

    target_local = near_tgt - my_base
    target_hot = (target_local[:, None] == jnp.arange(clusters_here)[None, :]).astype(jnp.float32)
    relative = (near_src // clusters_here - my_index) % peer_count
    slot = jnp.where(relative == 0, 0, jnp.where(relative == 1, 1, 2))
    near_index = slot * clusters_here + near_src % clusters_here
    near_pick = (near_index[:, None] == jnp.arange(3 * clusters_here)[None, :]).astype(jnp.bfloat16)

    far_local = far_src - my_base
    far_hot = (far_tgt[:, None] == jnp.arange(cluster_count)[None, :]).astype(jnp.float32)
    far_pick = (far_local[:, None] == jnp.arange(clusters_here)[None, :]).astype(jnp.bfloat16)
    row_f32 = row_basis.astype(jnp.float32)
    iterate_size = rhs_here * leaf_size
    coef_size = rhs_here * rank_size

    iterate = (coefficients[degree_top] * source).astype(jnp.bfloat16)
    result = source
    scaled = None
    for step in range(degree_top):
        degree = degree_top - 1 - step
        with jax.named_scope("far_partial"):
            far_input = jnp.einsum(
                "jc,cm->jm",
                far_pick,
                iterate.reshape(clusters_here, iterate_size),
                preferred_element_type=jnp.bfloat16,
            ).reshape(far_pick.shape[0], rhs_here, leaf_size)
            coef = jnp.einsum(
                "jrl,jkl->jrk", far_input, col_basis, preferred_element_type=jnp.float32
            )
            coef = coef.reshape(coef.shape[0], coef_size)
            partial_value = jnp.einsum("jc,jm->cm", far_hot, coef, precision=lax.Precision.HIGHEST)
            partial_value = partial_value.reshape(peer_count, clusters_here, coef_size)
        with jax.named_scope("clus_exchange"):
            far_mine = partial_value[my_index]
            iterate_flat = iterate.reshape(clusters_here, iterate_size)
            from_minus = iterate
            from_plus = iterate
            for s in range(1, peer_count):
                outgoing = split_three(partial_value[(my_index + s) % peer_count])
                carries_iterate = s == 1 or s == peer_count - 1
                if carries_iterate:
                    outgoing = jnp.concatenate([iterate_flat, outgoing], axis=1)
                if s == 1 and scaled is None:
                    scales, outgoing = lax.optimization_barrier((coefficients, outgoing))
                    scaled = [scales[d] * source for d in range(degree_top)]
                    scaled[0] = scales[0] * rhs_field
                incoming = shift(outgoing, "clus", peer_count, s)
                if carries_iterate:
                    neighbour = incoming[:, :iterate_size]
                    neighbour = neighbour.reshape(clusters_here, rhs_here, leaf_size)
                    if s == 1:
                        from_minus = neighbour
                    if s == peer_count - 1:
                        from_plus = neighbour
                    incoming = incoming[:, iterate_size:]
                far_mine = far_mine + join_three(incoming)
        with jax.named_scope("near_partial"):
            extended = jnp.concatenate([iterate, from_plus, from_minus], axis=0)
            gathered = jnp.einsum(
                "jc,cm->jm",
                near_pick,
                extended.reshape(3 * clusters_here, iterate_size),
                preferred_element_type=jnp.bfloat16,
            ).reshape(near_pick.shape[0], rhs_here, leaf_size)
            contrib = jnp.einsum(
                "jrs,jts->jrt", gathered, near_blocks, preferred_element_type=jnp.float32
            )
            last = degree == 0
            if last:
                near_part = jnp.einsum(
                    "jc,jrt->rct", target_hot, contrib, precision=lax.Precision.HIGHEST
                ).reshape(rhs_here, clusters_here * leaf_size)
                far_mine = far_mine.reshape(clusters_here, rhs_here, rank_size)
                far_mine = far_mine.transpose(1, 0, 2).reshape(rhs_here, clusters_here * rank_size)
            else:
                contrib = contrib.reshape(contrib.shape[0], iterate_size)
                near_part = jnp.einsum(
                    "jc,jm->cm", target_hot, contrib, precision=lax.Precision.HIGHEST
                )
        with jax.named_scope("pair_sums"):
            if scaled is None:
                scaled = [coefficients[d] * source for d in range(degree_top)]
                scaled[0] = coefficients[0] * rhs_field
            if step == 0:
                scaled, near_part = lax.optimization_barrier((scaled, near_part))
            packed = jnp.concatenate([near_part, far_mine], axis=1)
            packed = pair_total(packed, pair_count, pair_index)
            if last:
                near_width = clusters_here * leaf_size
                near_sum = packed[:, :near_width]
                coef_sum = packed[:, near_width:].reshape(rhs_here, clusters_here, rank_size)
            else:
                near_sum = packed[:, :iterate_size].reshape(clusters_here, rhs_here, leaf_size)
                coef_sum = packed[:, iterate_size:].reshape(clusters_here, rhs_here, rank_size)
        with jax.named_scope("far_field"):
            if last:
                far_field = jnp.einsum(
                    "rck,ckl->rcl", coef_sum, row_f32, precision=lax.Precision.HIGHEST
                ).reshape(rhs_here, clusters_here * leaf_size)
            else:
                far_field = jnp.einsum(
                    "crk,ckl->crl", coef_sum, row_f32, precision=lax.Precision.HIGHEST
                )
        result = near_sum + far_field + scaled[degree]
        iterate = result.astype(jnp.bfloat16)
    if degree_top == 0:
        return rhs_field
    return result


def solution(mesh):
    return jax.shard_map(
        shards,
        mesh=mesh,
        in_specs=(
            P("rhs", ("groups", "clus")),
            P(),
            P(("groups", "clus", "pair"), None, None),
            P(("groups", "clus", "pair")),
            P(("groups", "clus", "pair")),
            P(("groups", "clus"), None, None),
            P(("groups", "clus", "pair"), None, None),
            P(("groups", "clus", "pair")),
            P(("groups", "clus", "pair")),
        ),
        out_specs=P("rhs", ("groups", "clus")),
        check_vma=False,
    )
```

```python
import jax
import jax.numpy as jnp
from jax import lax
from jax.sharding import PartitionSpec as P


def shift(value, axis, count, step):
    return lax.ppermute(value, axis, [(i, (i + step) % count) for i in range(count)])


def split_three(value):
    high = lax.reduce_precision(value, exponent_bits=8, mantissa_bits=7)
    rest = value - high
    middle = lax.reduce_precision(rest, exponent_bits=8, mantissa_bits=7)
    low = rest - middle
    parts = [high, middle, low]
    return jnp.concatenate([part.astype(jnp.bfloat16) for part in parts], axis=-1)


def join_three(parts):
    width = parts.shape[-1] // 3
    high, middle, low = (
        parts[..., k * width : (k + 1) * width].astype(jnp.float32) for k in range(3)
    )
    return (high + middle) + low


def pair_total(value, pair_count, pair_index):
    if pair_count == 1:
        return value
    if pair_count == 2:
        return value + shift(value, "pair", 2, 1)
    received = [value] + [shift(value, "pair", pair_count, s) for s in range(1, pair_count)]
    stacked = jnp.stack(received)
    order = (pair_index - jnp.arange(pair_count)) % pair_count
    canonical = stacked[order]
    total = canonical[0]
    for q in range(1, pair_count):
        total = total + canonical[q]
    return total


def shards(
    rhs_field, coefficients, near_blocks, near_tgt, near_src, row_basis, col_basis, far_src, far_tgt
):
    rhs_here = rhs_field.shape[0]
    clusters_here = row_basis.shape[0]
    rank_size = row_basis.shape[1]
    leaf_size = row_basis.shape[2]
    peer_count = lax.axis_size("clus")
    pair_count = lax.axis_size("pair")
    cluster_count = clusters_here * peer_count
    degree_top = coefficients.shape[0] - 1
    my_index = lax.axis_index("clus")
    pair_index = lax.axis_index("pair")
    my_base = my_index * clusters_here
    source = rhs_field.reshape(rhs_here, clusters_here, leaf_size).transpose(1, 0, 2)

    target_local = near_tgt - my_base
    target_hot = (target_local[:, None] == jnp.arange(clusters_here)[None, :]).astype(jnp.float32)
    relative = (near_src // clusters_here - my_index) % peer_count
    slot = jnp.where(relative == 0, 0, jnp.where(relative == 1, 1, 2))
    near_index = slot * clusters_here + near_src % clusters_here
    near_pick = (near_index[:, None] == jnp.arange(3 * clusters_here)[None, :]).astype(jnp.bfloat16)

    far_local = far_src - my_base
    far_hot = (far_tgt[:, None] == jnp.arange(cluster_count)[None, :]).astype(jnp.float32)
    far_pick = (far_local[:, None] == jnp.arange(clusters_here)[None, :]).astype(jnp.bfloat16)
    row_f32 = row_basis.astype(jnp.float32)
    iterate_size = rhs_here * leaf_size
    coef_size = rhs_here * rank_size

    iterate = (coefficients[degree_top] * source).astype(jnp.bfloat16)
    result = source
    scaled = None
    for step in range(degree_top):
        degree = degree_top - 1 - step
        with jax.named_scope("far_partial"):
            far_input = jnp.einsum(
                "jc,cm->jm",
                far_pick,
                iterate.reshape(clusters_here, iterate_size),
                preferred_element_type=jnp.bfloat16,
            ).reshape(far_pick.shape[0], rhs_here, leaf_size)
            coef = jnp.einsum(
                "jrl,jkl->jrk", far_input, col_basis, preferred_element_type=jnp.float32
            )
            coef = coef.reshape(coef.shape[0], coef_size)
            partial_value = jnp.einsum("jc,jm->cm", far_hot, coef, precision=lax.Precision.HIGHEST)
            partial_value = partial_value.reshape(peer_count, clusters_here, coef_size)
        with jax.named_scope("clus_exchange"):
            far_mine = partial_value[my_index]
            iterate_flat = iterate.reshape(clusters_here, iterate_size)
            from_minus = iterate
            from_plus = iterate
            long_shifts = sorted({1, peer_count - 1}) if peer_count > 1 else []
            short_shifts = list(range(2, peer_count - 1))
            for s in long_shifts:
                outgoing = split_three(partial_value[(my_index + s) % peer_count])
                outgoing = jnp.concatenate([iterate_flat, outgoing], axis=1)
                if s == 1 and scaled is None:
                    scales, outgoing = lax.optimization_barrier((coefficients, outgoing))
                    scaled = [scales[d] * source for d in range(degree_top)]
                incoming = shift(outgoing, "clus", peer_count, s)
                neighbour = incoming[:, :iterate_size]
                neighbour = neighbour.reshape(clusters_here, rhs_here, leaf_size)
                if s == 1:
                    from_minus = neighbour
                if s == peer_count - 1:
                    from_plus = neighbour
                far_mine = far_mine + join_three(incoming[:, iterate_size:])
            if short_shifts:
                far_pair = pair_total(partial_value, pair_count, pair_index)
        with jax.named_scope("near_partial"):
            extended = jnp.concatenate([iterate, from_plus, from_minus], axis=0)
            gathered = jnp.einsum(
                "jc,cm->jm",
                near_pick,
                extended.reshape(3 * clusters_here, iterate_size),
                preferred_element_type=jnp.bfloat16,
            ).reshape(near_pick.shape[0], rhs_here, leaf_size)
            contrib = jnp.einsum(
                "jrs,jts->jrt", gathered, near_blocks, preferred_element_type=jnp.float32
            )
            contrib = contrib.reshape(contrib.shape[0], iterate_size)
            near_part = jnp.einsum(
                "jc,jm->cm", target_hot, contrib, precision=lax.Precision.HIGHEST
            )
        with jax.named_scope("pair_sums"):
            if scaled is None:
                scaled = [coefficients[d] * source for d in range(degree_top)]
            if step == 0:
                scaled, near_part = lax.optimization_barrier((scaled, near_part))
            packed = jnp.concatenate([near_part, far_mine], axis=1)
            packed = pair_total(packed, pair_count, pair_index)
            near_sum = packed[:, :iterate_size].reshape(clusters_here, rhs_here, leaf_size)
            coef_flat = packed[:, iterate_size:]
            for s in short_shifts:
                coef_flat = coef_flat + shift(
                    far_pair[(my_index + s) % peer_count], "clus", peer_count, s
                )
            coef_sum = coef_flat.reshape(clusters_here, rhs_here, rank_size)
        with jax.named_scope("far_field"):
            far_field = jnp.einsum(
                "crk,ckl->crl", coef_sum, row_f32, precision=lax.Precision.HIGHEST
            )
        result = near_sum + far_field + scaled[degree]
        iterate = result.astype(jnp.bfloat16)
    return result.transpose(1, 0, 2).reshape(rhs_here, clusters_here * leaf_size)


def solution(mesh):
    return jax.shard_map(
        shards,
        mesh=mesh,
        in_specs=(
            P("rhs", ("groups", "clus")),
            P(),
            P(("groups", "clus", "pair"), None, None),
            P(("groups", "clus", "pair")),
            P(("groups", "clus", "pair")),
            P(("groups", "clus"), None, None),
            P(("groups", "clus", "pair"), None, None),
            P(("groups", "clus", "pair")),
            P(("groups", "clus", "pair")),
        ),
        out_specs=P("rhs", ("groups", "clus")),
        check_vma=False,
    )
```

```python
import jax
import jax.numpy as jnp
from jax import lax
from jax.sharding import PartitionSpec as P


def shift(value, axis, count, step):
    return lax.ppermute(value, axis, [(i, (i + step) % count) for i in range(count)])


def split_three(value):
    high = lax.reduce_precision(value, exponent_bits=8, mantissa_bits=7)
    rest = value - high
    middle = lax.reduce_precision(rest, exponent_bits=8, mantissa_bits=7)
    low = rest - middle
    parts = [high, middle, low]
    return jnp.concatenate([part.astype(jnp.bfloat16) for part in parts], axis=-1)


def join_three(parts):
    width = parts.shape[-1] // 3
    high, middle, low = (
        parts[..., k * width : (k + 1) * width].astype(jnp.float32) for k in range(3)
    )
    return (high + middle) + low


def pair_total(value, pair_count, pair_index):
    if pair_count == 1:
        return value
    if pair_count == 2:
        return value + shift(value, "pair", 2, 1)
    received = [value] + [shift(value, "pair", pair_count, s) for s in range(1, pair_count)]
    stacked = jnp.stack(received)
    order = (pair_index - jnp.arange(pair_count)) % pair_count
    canonical = stacked[order]
    total = canonical[0]
    for q in range(1, pair_count):
        total = total + canonical[q]
    return total


def shards(
    rhs_field, coefficients, near_blocks, near_tgt, near_src, row_basis, col_basis, far_src, far_tgt
):
    rhs_here = rhs_field.shape[0]
    clusters_here = row_basis.shape[0]
    rank_size = row_basis.shape[1]
    leaf_size = row_basis.shape[2]
    peer_count = lax.axis_size("clus")
    pair_count = lax.axis_size("pair")
    cluster_count = clusters_here * peer_count
    degree_top = coefficients.shape[0] - 1
    my_index = lax.axis_index("clus")
    pair_index = lax.axis_index("pair")
    my_base = my_index * clusters_here
    source = rhs_field.reshape(rhs_here, clusters_here, leaf_size).transpose(1, 0, 2)

    target_local = near_tgt - my_base
    target_hot = (target_local[:, None] == jnp.arange(clusters_here)[None, :]).astype(jnp.float32)
    relative = (near_src // clusters_here - my_index) % peer_count
    slot = jnp.where(relative == 0, 0, jnp.where(relative == 1, 1, 2))
    near_index = slot * clusters_here + near_src % clusters_here
    near_pick = (near_index[:, None] == jnp.arange(3 * clusters_here)[None, :]).astype(jnp.bfloat16)

    far_local = far_src - my_base
    far_hot = (far_tgt[:, None] == jnp.arange(cluster_count)[None, :]).astype(jnp.float32)
    far_pick = (far_local[:, None] == jnp.arange(clusters_here)[None, :]).astype(jnp.bfloat16)
    row_f32 = row_basis.astype(jnp.float32)
    iterate_size = rhs_here * leaf_size
    coef_size = rhs_here * rank_size

    iterate = (coefficients[degree_top] * source).astype(jnp.bfloat16)
    result = source
    scaled = None
    for step in range(degree_top):
        degree = degree_top - 1 - step
        with jax.named_scope("far_partial"):
            far_input = jnp.einsum(
                "jc,cm->jm",
                far_pick,
                iterate.reshape(clusters_here, iterate_size),
                preferred_element_type=jnp.bfloat16,
            ).reshape(far_pick.shape[0], rhs_here, leaf_size)
            coef = jnp.einsum(
                "jrl,jkl->jrk", far_input, col_basis, preferred_element_type=jnp.float32
            )
            coef = coef.reshape(coef.shape[0], coef_size)
            partial_value = jnp.einsum("jc,jm->cm", far_hot, coef, precision=lax.Precision.HIGHEST)
            partial_value = partial_value.reshape(peer_count, clusters_here, coef_size)
        with jax.named_scope("clus_exchange"):
            far_mine = partial_value[my_index]
            iterate_flat = iterate.reshape(clusters_here, iterate_size)
            from_minus = iterate
            from_plus = iterate
            long_shifts = sorted({1, peer_count - 1}) if peer_count > 1 else []
            short_shifts = list(range(2, peer_count - 1))
            for s in long_shifts:
                outgoing = split_three(partial_value[(my_index + s) % peer_count])
                outgoing = jnp.concatenate([iterate_flat, outgoing], axis=1)
                if s == 1 and scaled is None:
                    scales, outgoing = lax.optimization_barrier((coefficients, outgoing))
                    scaled = [scales[d] * source for d in range(degree_top)]
                incoming = shift(outgoing, "clus", peer_count, s)
                neighbour = incoming[:, :iterate_size]
                neighbour = neighbour.reshape(clusters_here, rhs_here, leaf_size)
                if s == 1:
                    from_minus = neighbour
                if s == peer_count - 1:
                    from_plus = neighbour
                far_mine = far_mine + join_three(incoming[:, iterate_size:])
            if short_shifts:
                far_far = jnp.stack(
                    [partial_value[(my_index + s) % peer_count] for s in short_shifts]
                )
                far_pair = pair_total(far_far, pair_count, pair_index)
        with jax.named_scope("near_partial"):
            extended = jnp.concatenate([iterate, from_plus, from_minus], axis=0)
            gathered = jnp.einsum(
                "jc,cm->jm",
                near_pick,
                extended.reshape(3 * clusters_here, iterate_size),
                preferred_element_type=jnp.bfloat16,
            ).reshape(near_pick.shape[0], rhs_here, leaf_size)
            contrib = jnp.einsum(
                "jrs,jts->jrt", gathered, near_blocks, preferred_element_type=jnp.float32
            )
            contrib = contrib.reshape(contrib.shape[0], iterate_size)
            near_part = jnp.einsum(
                "jc,jm->cm", target_hot, contrib, precision=lax.Precision.HIGHEST
            )
        with jax.named_scope("pair_sums"):
            if scaled is None:
                scaled = [coefficients[d] * source for d in range(degree_top)]
            if step == 0:
                scaled, near_part = lax.optimization_barrier((scaled, near_part))
            packed = jnp.concatenate([near_part, far_mine], axis=1)
            packed = pair_total(packed, pair_count, pair_index)
            near_sum = packed[:, :iterate_size].reshape(clusters_here, rhs_here, leaf_size)
            coef_flat = packed[:, iterate_size:]
            for k, s in enumerate(short_shifts):
                coef_flat = coef_flat + shift(far_pair[k], "clus", peer_count, s)
            coef_sum = coef_flat.reshape(clusters_here, rhs_here, rank_size)
        with jax.named_scope("far_field"):
            far_field = jnp.einsum(
                "crk,ckl->crl", coef_sum, row_f32, precision=lax.Precision.HIGHEST
            )
        result = near_sum + far_field + scaled[degree]
        iterate = result.astype(jnp.bfloat16)
    return result.transpose(1, 0, 2).reshape(rhs_here, clusters_here * leaf_size)


def solution(mesh):
    return jax.shard_map(
        shards,
        mesh=mesh,
        in_specs=(
            P("rhs", ("groups", "clus")),
            P(),
            P(("groups", "clus", "pair"), None, None),
            P(("groups", "clus", "pair")),
            P(("groups", "clus", "pair")),
            P(("groups", "clus"), None, None),
            P(("groups", "clus", "pair"), None, None),
            P(("groups", "clus", "pair")),
            P(("groups", "clus", "pair")),
        ),
        out_specs=P("rhs", ("groups", "clus")),
        check_vma=False,
    )
```

```python
import jax
import jax.numpy as jnp
from jax import lax
from jax.sharding import PartitionSpec as P


def shift(value, axis, count, step):
    return lax.ppermute(value, axis, [(i, (i + step) % count) for i in range(count)])


def split_three(value):
    high = lax.reduce_precision(value, exponent_bits=8, mantissa_bits=7)
    rest = value - high
    middle = lax.reduce_precision(rest, exponent_bits=8, mantissa_bits=7)
    low = rest - middle
    parts = [high, middle, low]
    return jnp.concatenate([part.astype(jnp.bfloat16) for part in parts], axis=-1)


def join_three(parts):
    width = parts.shape[-1] // 3
    high, middle, low = (
        parts[..., k * width : (k + 1) * width].astype(jnp.float32) for k in range(3)
    )
    return (high + middle) + low


def pair_total(value, pair_count, pair_index):
    if pair_count == 1:
        return value
    if pair_count == 2:
        return value + shift(value, "pair", 2, 1)
    received = [value] + [shift(value, "pair", pair_count, s) for s in range(1, pair_count)]
    stacked = jnp.stack(received)
    order = (pair_index - jnp.arange(pair_count)) % pair_count
    canonical = stacked[order]
    total = canonical[0]
    for q in range(1, pair_count):
        total = total + canonical[q]
    return total


def pair_total_list(arrivals, pair_index):
    pair_count = len(arrivals)
    if pair_count == 1:
        return arrivals[0]
    if pair_count == 2:
        return arrivals[0] + arrivals[1]
    stacked = jnp.stack(arrivals)
    order = (pair_index - jnp.arange(pair_count)) % pair_count
    canonical = stacked[order]
    total = canonical[0]
    for q in range(1, pair_count):
        total = total + canonical[q]
    return total


def shards(
    rhs_field, coefficients, near_blocks, near_tgt, near_src, row_basis, col_basis, far_src, far_tgt
):
    rhs_here = rhs_field.shape[0]
    clusters_here = row_basis.shape[0]
    rank_size = row_basis.shape[1]
    leaf_size = row_basis.shape[2]
    peer_count = lax.axis_size("clus")
    pair_count = lax.axis_size("pair")
    cluster_count = clusters_here * peer_count
    degree_top = coefficients.shape[0] - 1
    my_index = lax.axis_index("clus")
    pair_index = lax.axis_index("pair")
    my_base = my_index * clusters_here
    source = rhs_field.reshape(rhs_here, clusters_here, leaf_size).transpose(1, 0, 2)

    target_local = near_tgt - my_base
    target_hot = (target_local[:, None] == jnp.arange(clusters_here)[None, :]).astype(jnp.float32)
    relative = (near_src // clusters_here - my_index) % peer_count
    slot = jnp.where(relative == 0, 0, jnp.where(relative == 1, 1, 2))
    near_index = slot * clusters_here + near_src % clusters_here
    near_pick = (near_index[:, None] == jnp.arange(3 * clusters_here)[None, :]).astype(jnp.bfloat16)

    far_local = far_src - my_base
    far_hot = (far_tgt[:, None] == jnp.arange(cluster_count)[None, :]).astype(jnp.float32)
    far_pick = (far_local[:, None] == jnp.arange(clusters_here)[None, :]).astype(jnp.bfloat16)
    row_f32 = row_basis.astype(jnp.float32)
    iterate_size = rhs_here * leaf_size
    coef_size = rhs_here * rank_size

    iterate = (coefficients[degree_top] * source).astype(jnp.bfloat16)
    result = source
    scaled = None
    for step in range(degree_top):
        degree = degree_top - 1 - step
        with jax.named_scope("far_partial"):
            far_input = jnp.einsum(
                "jc,cm->jm",
                far_pick,
                iterate.reshape(clusters_here, iterate_size),
                preferred_element_type=jnp.bfloat16,
            ).reshape(far_pick.shape[0], rhs_here, leaf_size)
            coef = jnp.einsum(
                "jrl,jkl->jrk", far_input, col_basis, preferred_element_type=jnp.float32
            )
            coef = coef.reshape(coef.shape[0], coef_size)
            partial_value = jnp.einsum("jc,jm->cm", far_hot, coef, precision=lax.Precision.HIGHEST)
            partial_value = partial_value.reshape(peer_count, clusters_here, coef_size)
        with jax.named_scope("clus_exchange"):
            far_mine = partial_value[my_index]
            iterate_flat = iterate.reshape(clusters_here, iterate_size)
            from_minus = iterate
            from_plus = iterate
            long_shifts = sorted({1, peer_count - 1}) if peer_count > 1 else []
            short_shifts = list(range(2, peer_count - 1))
            for s in long_shifts:
                outgoing = split_three(partial_value[(my_index + s) % peer_count])
                outgoing = jnp.concatenate([iterate_flat, outgoing], axis=1)
                if s == 1 and scaled is None:
                    scales, outgoing = lax.optimization_barrier((coefficients, outgoing))
                    scaled = [scales[d] * source for d in range(degree_top)]
                incoming = shift(outgoing, "clus", peer_count, s)
                neighbour = incoming[:, :iterate_size]
                neighbour = neighbour.reshape(clusters_here, rhs_here, leaf_size)
                if s == 1:
                    from_minus = neighbour
                if s == peer_count - 1:
                    from_plus = neighbour
                far_mine = far_mine + join_three(incoming[:, iterate_size:])
        with jax.named_scope("near_partial"):
            extended = jnp.concatenate([iterate, from_plus, from_minus], axis=0)
            gathered = jnp.einsum(
                "jc,cm->jm",
                near_pick,
                extended.reshape(3 * clusters_here, iterate_size),
                preferred_element_type=jnp.bfloat16,
            ).reshape(near_pick.shape[0], rhs_here, leaf_size)
            contrib = jnp.einsum(
                "jrs,jts->jrt", gathered, near_blocks, preferred_element_type=jnp.float32
            )
            contrib = contrib.reshape(contrib.shape[0], iterate_size)
            near_part = jnp.einsum(
                "jc,jm->cm", target_hot, contrib, precision=lax.Precision.HIGHEST
            )
        with jax.named_scope("pair_sums"):
            if scaled is None:
                scaled = [coefficients[d] * source for d in range(degree_top)]
            if step == 0:
                scaled, near_part = lax.optimization_barrier((scaled, near_part))
            packed = jnp.concatenate([near_part, far_mine], axis=1)
            packed = pair_total(packed, pair_count, pair_index)
            near_sum = packed[:, :iterate_size].reshape(clusters_here, rhs_here, leaf_size)
            coef_flat = packed[:, iterate_size:]
            for s in short_shifts:
                outgoing = partial_value[(my_index + s) % peer_count]
                arrivals = []
                for t in range(pair_count):
                    pairs = [
                        (c * pair_count + p, ((c + s) % peer_count) * pair_count + (p + t) % pair_count)
                        for c in range(peer_count)
                        for p in range(pair_count)
                    ]
                    arrivals.append(lax.ppermute(outgoing, ("clus", "pair"), pairs))
                coef_flat = coef_flat + pair_total_list(arrivals, pair_index)
            coef_sum = coef_flat.reshape(clusters_here, rhs_here, rank_size)
        with jax.named_scope("far_field"):
            far_field = jnp.einsum(
                "crk,ckl->crl", coef_sum, row_f32, precision=lax.Precision.HIGHEST
            )
        result = near_sum + far_field + scaled[degree]
        iterate = result.astype(jnp.bfloat16)
    return result.transpose(1, 0, 2).reshape(rhs_here, clusters_here * leaf_size)


def solution(mesh):
    return jax.shard_map(
        shards,
        mesh=mesh,
        in_specs=(
            P("rhs", ("groups", "clus")),
            P(),
            P(("groups", "clus", "pair"), None, None),
            P(("groups", "clus", "pair")),
            P(("groups", "clus", "pair")),
            P(("groups", "clus"), None, None),
            P(("groups", "clus", "pair"), None, None),
            P(("groups", "clus", "pair")),
            P(("groups", "clus", "pair")),
        ),
        out_specs=P("rhs", ("groups", "clus")),
        check_vma=False,
    )
```

```python
import jax
import jax.numpy as jnp
from jax import lax
from jax.sharding import PartitionSpec as P


def shift(value, axis, count, step):
    return lax.ppermute(value, axis, [(i, (i + step) % count) for i in range(count)])


def split_three(value):
    high = lax.reduce_precision(value, exponent_bits=8, mantissa_bits=7)
    rest = value - high
    middle = lax.reduce_precision(rest, exponent_bits=8, mantissa_bits=7)
    low = rest - middle
    parts = [high, middle, low]
    return jnp.concatenate([part.astype(jnp.bfloat16) for part in parts], axis=-1)


def join_three(parts):
    width = parts.shape[-1] // 3
    high, middle, low = (
        parts[..., k * width : (k + 1) * width].astype(jnp.float32) for k in range(3)
    )
    return (high + middle) + low


def one_hot_sum(hot, values):
    summed = jnp.einsum(
        "jc,jm->cm", hot.astype(jnp.bfloat16), split_three(values),
        preferred_element_type=jnp.float32,
    )
    width = values.shape[-1]
    return (summed[:, :width] + summed[:, width : 2 * width]) + summed[:, 2 * width :]


def pair_total(value, pair_count, pair_index):
    if pair_count == 1:
        return value
    if pair_count == 2:
        return value + shift(value, "pair", 2, 1)
    received = [value] + [shift(value, "pair", pair_count, s) for s in range(1, pair_count)]
    stacked = jnp.stack(received)
    order = (pair_index - jnp.arange(pair_count)) % pair_count
    canonical = stacked[order]
    total = canonical[0]
    for q in range(1, pair_count):
        total = total + canonical[q]
    return total


def shards(
    rhs_field, coefficients, near_blocks, near_tgt, near_src, row_basis, col_basis, far_src, far_tgt
):
    rhs_here = rhs_field.shape[0]
    clusters_here = row_basis.shape[0]
    rank_size = row_basis.shape[1]
    leaf_size = row_basis.shape[2]
    peer_count = lax.axis_size("clus")
    pair_count = lax.axis_size("pair")
    cluster_count = clusters_here * peer_count
    degree_top = coefficients.shape[0] - 1
    my_index = lax.axis_index("clus")
    pair_index = lax.axis_index("pair")
    my_base = my_index * clusters_here
    source = rhs_field.reshape(rhs_here, clusters_here, leaf_size).transpose(1, 0, 2)

    target_local = near_tgt - my_base
    target_hot = (target_local[:, None] == jnp.arange(clusters_here)[None, :]).astype(jnp.float32)
    relative = (near_src // clusters_here - my_index) % peer_count
    slot = jnp.where(relative == 0, 0, jnp.where(relative == 1, 1, 2))
    near_index = slot * clusters_here + near_src % clusters_here
    near_pick = (near_index[:, None] == jnp.arange(3 * clusters_here)[None, :]).astype(jnp.bfloat16)

    far_local = far_src - my_base
    far_hot = (far_tgt[:, None] == jnp.arange(cluster_count)[None, :]).astype(jnp.float32)
    far_pick = (far_local[:, None] == jnp.arange(clusters_here)[None, :]).astype(jnp.bfloat16)
    row_f32 = row_basis.astype(jnp.float32)
    iterate_size = rhs_here * leaf_size
    coef_size = rhs_here * rank_size

    iterate = (coefficients[degree_top] * source).astype(jnp.bfloat16)
    result = source
    scaled = None
    for step in range(degree_top):
        degree = degree_top - 1 - step
        with jax.named_scope("far_partial"):
            far_input = jnp.einsum(
                "jc,cm->jm",
                far_pick,
                iterate.reshape(clusters_here, iterate_size),
                preferred_element_type=jnp.bfloat16,
            ).reshape(far_pick.shape[0], rhs_here, leaf_size)
            coef = jnp.einsum(
                "jrl,jkl->jrk", far_input, col_basis, preferred_element_type=jnp.float32
            )
            coef = coef.reshape(coef.shape[0], coef_size)
            partial_value = one_hot_sum(far_hot, coef)
            partial_value = partial_value.reshape(peer_count, clusters_here, coef_size)
        with jax.named_scope("clus_exchange"):
            far_mine = partial_value[my_index]
            iterate_flat = iterate.reshape(clusters_here, iterate_size)
            from_minus = iterate
            from_plus = iterate
            long_shifts = sorted({1, peer_count - 1}) if peer_count > 1 else []
            short_shifts = list(range(2, peer_count - 1))
            for s in long_shifts:
                outgoing = split_three(partial_value[(my_index + s) % peer_count])
                outgoing = jnp.concatenate([iterate_flat, outgoing], axis=1)
                if s == 1 and scaled is None:
                    scales, outgoing = lax.optimization_barrier((coefficients, outgoing))
                    scaled = [scales[d] * source for d in range(degree_top)]
                incoming = shift(outgoing, "clus", peer_count, s)
                neighbour = incoming[:, :iterate_size]
                neighbour = neighbour.reshape(clusters_here, rhs_here, leaf_size)
                if s == 1:
                    from_minus = neighbour
                if s == peer_count - 1:
                    from_plus = neighbour
                far_mine = far_mine + join_three(incoming[:, iterate_size:])
            if short_shifts:
                far_far = jnp.stack(
                    [partial_value[(my_index + s) % peer_count] for s in short_shifts]
                )
                far_pair = pair_total(far_far, pair_count, pair_index)
        with jax.named_scope("near_partial"):
            extended = jnp.concatenate([iterate, from_plus, from_minus], axis=0)
            gathered = jnp.einsum(
                "jc,cm->jm",
                near_pick,
                extended.reshape(3 * clusters_here, iterate_size),
                preferred_element_type=jnp.bfloat16,
            ).reshape(near_pick.shape[0], rhs_here, leaf_size)
            contrib = jnp.einsum(
                "jrs,jts->jrt", gathered, near_blocks, preferred_element_type=jnp.float32
            )
            contrib = contrib.reshape(contrib.shape[0], iterate_size)
            near_part = one_hot_sum(target_hot, contrib)
        with jax.named_scope("pair_sums"):
            if scaled is None:
                scaled = [coefficients[d] * source for d in range(degree_top)]
            if step == 0:
                scaled, near_part = lax.optimization_barrier((scaled, near_part))
            packed = jnp.concatenate([near_part, far_mine], axis=1)
            packed = pair_total(packed, pair_count, pair_index)
            near_sum = packed[:, :iterate_size].reshape(clusters_here, rhs_here, leaf_size)
            coef_flat = packed[:, iterate_size:]
            for k, s in enumerate(short_shifts):
                coef_flat = coef_flat + shift(far_pair[k], "clus", peer_count, s)
            coef_sum = coef_flat.reshape(clusters_here, rhs_here, rank_size)
        with jax.named_scope("far_field"):
            far_field = jnp.einsum(
                "crk,ckl->crl", coef_sum, row_f32, precision=lax.Precision.HIGHEST
            )
        result = near_sum + far_field + scaled[degree]
        iterate = result.astype(jnp.bfloat16)
    return result.transpose(1, 0, 2).reshape(rhs_here, clusters_here * leaf_size)


def solution(mesh):
    return jax.shard_map(
        shards,
        mesh=mesh,
        in_specs=(
            P("rhs", ("groups", "clus")),
            P(),
            P(("groups", "clus", "pair"), None, None),
            P(("groups", "clus", "pair")),
            P(("groups", "clus", "pair")),
            P(("groups", "clus"), None, None),
            P(("groups", "clus", "pair"), None, None),
            P(("groups", "clus", "pair")),
            P(("groups", "clus", "pair")),
        ),
        out_specs=P("rhs", ("groups", "clus")),
        check_vma=False,
    )
```
